128 devices in a mesh: dp: 16 (over z, y_lo, core), mp: 8 (over x, y_hi).
Axes of the slice: x: 4, y: 4 (y_hi: 2, y_lo: 2; y = y_hi * 2 + y_lo), z: 4, core: 2. Of those that a mesh axis runs over, the one named last changes fastest.
Arguments:
- hidden: bfloat16 [6144, 8192], P('dp', 'mp'), may hold values from -1000 to 1000
- norm_gain: bfloat16 [8192], replicated, may hold values from 0.099609375 to 1.8984375
- query_weight: bfloat16 [8192, 8192], P('dp', 'mp'), may hold values from -0.0625 to 0.0625
- key_weight: bfloat16 [8192, 1024], P('dp', 'mp'), may hold values from -0.0625 to 0.0625
- value_weight: bfloat16 [8192, 1024], P('dp', 'mp'), may hold values from -0.0625 to 0.0625
- query_bias: bfloat16 [8192], P('mp'), may hold values from -3 to 3
- key_bias: bfloat16 [1024], P('mp'), may hold values from -3 to 3
- value_bias: bfloat16 [1024], P('mp'), may hold values from -3 to 3
- request_lens: int32 [3], replicated, may hold values from 1 to 3072, 6144 in all
- request_group: int32 [3], replicated, may hold values from 0 to 3
- prompt_lens: int32 [4], replicated, may hold values from 1 to 512, 1280 in all
- prompt_table: int32 [4, 4], replicated, may hold values from 0 to 15, as said below
- pool_keys: bfloat16 [16, 128, 1024], P('dp', None, 'mp'), may hold values from -1000 to 1000
- pool_values: bfloat16 [16, 128, 1024], P('dp', None, 'mp'), may hold values from -6 to 6
- prev_cache: bfloat16 [256, 4, 2, 128, 1024], P('dp', None, None, None, 'mp'), may hold values from -6 to 6
- dest_device: int32 [256, 1], P('dp'), may hold values from 0 to 15, as said below
Outputs:
- context: bfloat16 [6144, 8192], P('dp', 'mp')
- decode_cache: bfloat16 [256, 4, 2, 128, 1024], P('dp', None, None, None, 'mp')
The draws below stay inside these ranges and needn't reach their ends.
Inputs may be any that keep to these rules, and one draw needn't show every extreme that they name: `request_lens`: requests are packed back to back in this order and sum to 6144. `prompt_table`: every pool block is named exactly once. `dest_device`: of the 16 blocks of one index of dp at most 2 name the same device, and every device is named by exactly 16 blocks in all.
All inputs are finite; a program needn't handle non-finite values.
Results may differ from the reference program's by a relative error of at most 0.03.
Values may be sent and summed in bfloat16 or wider, within the bound.
No kernel may reach another device: no remote copies, remote signals or barrier semaphores. Data moves between devices by JAX's collectives and lax.ppermute only.
A program may use at most 192 MiB of HBM per device.

```python
import math
import jax
import jax.numpy as jnp
import numpy as np
from jax import lax

D = 8192
QH = 64
KV = 8
HD = 128
BS = 128
PBLK = 4
BLK_DEV = 16
CL = 4
REQS = 3
TOKENS = 6144
POOL_BLK = 16
GROUPS = 4
NBLK = 256
N_DP = 16


def draw_hidden(key, part):
    key_base, key_rows, key_cols = jax.random.split(key, 3)
    base_part = jax.random.truncated_normal(key_base, -4.0, 4.0, (TOKENS, D), jnp.float32)
    row_scale = jnp.exp(jax.random.uniform(key_rows, (TOKENS, 1), jnp.float32, 0.0, math.log(10.0)))
    col_scale = jnp.exp(jax.random.uniform(key_cols, (1, D), jnp.float32, 0.0, math.log(10.0)))
    return (base_part * row_scale * col_scale).astype(jnp.bfloat16)


def draw_pool_keys(key, part):
    key_width = KV * HD
    key_base = jax.random.fold_in(key, 0)
    values = jax.random.truncated_normal(key_base, -4.0, 4.0, (POOL_BLK, BS, key_width), jnp.float32)
    return values.astype(jnp.bfloat16)


def draw_prompt_table(key, part):
    return jax.random.permutation(key, POOL_BLK).astype(jnp.int32).reshape(GROUPS, PBLK)


def draw_dest_device(key, part):
    devices = NBLK // BLK_DEV
    key_twin, key_rest, key_order, key_label = jax.random.split(key, 4)
    twin_shift = jax.random.randint(key_twin, (1,), 0, devices, dtype=jnp.int32)
    spare_shifts = jax.random.permutation(key_rest, 2 * (devices - 1)).astype(jnp.int32) % (devices - 1)
    others = (twin_shift + 1 + spare_shifts[:BLK_DEV - 2]) % devices
    shifts = jnp.concatenate([twin_shift, twin_shift, others])
    scores = jax.random.randint(key_order, (devices, BLK_DEV), 0, 1 << 20, dtype=jnp.int32) * BLK_DEV + jnp.arange(BLK_DEV, dtype=jnp.int32)[None, :]
    slot_order = jnp.argsort(scores, axis=1)
    labels = jax.random.permutation(key_label, devices).astype(jnp.int32)
    senders = jnp.arange(devices, dtype=jnp.int32)[:, None]
    target = labels[(senders + shifts[slot_order]) % devices]
    return target.reshape(NBLK, 1).astype(jnp.int32)


def block_scale(stream_key, extent, shards, low, high):
    def one(position, blocks):
        heights = jax.random.uniform(jax.random.fold_in(jax.random.fold_in(stream_key, 6), position), (blocks,), jnp.float32, low / len(shards), high / len(shards))
        return jnp.repeat(jnp.exp(heights), extent[position] // blocks).reshape((-1,) + (1,) * (len(extent) - position - 1))

    factor_of = one(*shards[0])
    for cut in shards[1:]:
        factor_of = factor_of * one(*cut)
    return factor_of


def length_profile(amount, total, most, skew):
    weights = [(1 << 20) // math.isqrt(grade ** skew) + 1 for grade in range(2, amount + 1)]
    rest, counts = total - most - (amount - 1), [1] * (amount - 1)
    while rest > 0:
        candidates = [i for i in range(amount - 1) if counts[i] < most]
        whole, budget = sum([weights[i] for i in candidates]), rest
        for i in candidates:
            more = min(most - counts[i], max(1, budget * weights[i] // whole), rest)
            counts[i] = counts[i] + more
            rest = rest - more
    return np.array([most] + counts)


def uneven(stream_key, number_of, total, limit, slope):
    if number_of == 2:
        one = jax.random.randint(stream_key, (), max(1, total - limit), min(limit, total - 1) + 1)
        return jnp.stack([one, total - one])
    tallies = jnp.asarray(length_profile(number_of, total, limit, slope), jnp.int32)
    twos = (number_of - 1) // 2
    donor, sink = tallies[1:1 + 2 * twos:2], tallies[2:2 + 2 * twos:2]
    margin = jnp.minimum(donor - 1, limit - sink)
    passed = jax.random.randint(jax.random.fold_in(stream_key, 1), (twos,), 0, 1 << 20) % (margin + 1)
    tallies = tallies.at[1:1 + 2 * twos:2].set(donor - passed).at[2:2 + 2 * twos:2].set(sink + passed)
    return tallies[jax.random.permutation(jax.random.fold_in(stream_key, 2), number_of)]


def normal_values(own_key, shape, spread, bound, cuts=(), held_as=jnp.bfloat16):
    entries = jax.random.normal(own_key, shape, jnp.float32) * spread
    if len(cuts) > 0:
        entries = block_scale(own_key, shape, cuts, -0.22, 0.18) * entries
    return jnp.clip(entries, min=-bound, max=bound).astype(held_as)


def setup_inputs(seed: int = 0) -> dict:
    key_list = jax.random.split(jax.random.key(seed), 17)
    return {
        "hidden": draw_hidden(jax.random.fold_in(key_list[16], 71), 0),
        "norm_gain": jnp.clip(1.0 + 0.18 * jax.random.normal(key_list[1], (D,), jnp.float32), 0.099609375, 1.8984375).astype(jnp.bfloat16),
        "query_weight": normal_values(key_list[2], (D, QH * HD), D ** -0.5, 0.0625, ((0, 16), (1, 8))),
        "key_weight": normal_values(key_list[3], (D, KV * HD), D ** -0.5, 0.0625, ((0, 16), (1, 8))),
        "value_weight": normal_values(key_list[4], (D, KV * HD), D ** -0.5, 0.0625, ((0, 16), (1, 8))),
        "query_bias": normal_values(key_list[5], (QH * HD,), 0.5, 3.0, ((0, 8),)),
        "key_bias": normal_values(key_list[6], (KV * HD,), 0.5, 3.0, ((0, 8),)),
        "value_bias": normal_values(key_list[7], (KV * HD,), 0.5, 3.0, ((0, 8),)),
        "request_lens": uneven(key_list[8], REQS, TOKENS, TOKENS // 2, 2).astype(jnp.int32),
        "request_group": jax.random.randint(key_list[9], (REQS,), 0, GROUPS).astype(jnp.int32),
        "prompt_lens": uneven(key_list[10], GROUPS, GROUPS * PBLK * BS * 5 // 8, PBLK * BS, 1).astype(jnp.int32),
        "prompt_table": draw_prompt_table(jax.random.fold_in(key_list[16], 71), 0),
        "pool_keys": draw_pool_keys(jax.random.fold_in(key_list[16], 71), 0),
        "pool_values": normal_values(key_list[13], (POOL_BLK, BS, KV * HD), 1.0, 6.0, ((0, 16), (2, 8))),
        "prev_cache": normal_values(key_list[14], (NBLK, CL, 2, BS, KV * HD), 1.0, 6.0, ((0, 16), (4, 8))),
        "dest_device": draw_dest_device(jax.random.fold_in(key_list[16], 71), 0),
    }


NEG_BIG = -1e+30
EPSILON = 1e-06
THETA = 1000000.0

def rotary(values, positions):
    head_dim = values.shape[-1]
    half_dim = head_dim // 2
    frequency = jnp.exp(-jnp.arange(half_dim, dtype=jnp.float32) * (2.0 / head_dim) * math.log(THETA))
    angles = positions[:, None] * frequency[None, :]
    cosine = jnp.concatenate([jnp.cos(angles), jnp.cos(angles)], axis=-1)[:, None, :]
    sine_part = jnp.concatenate([jnp.sin(angles), jnp.sin(angles)], axis=-1)[:, None, :]
    first_half = values[..., :half_dim]
    second_half = values[..., half_dim:]
    turned = jnp.concatenate([-second_half, first_half], axis=-1)
    return values * cosine + turned * sine_part

def request_index(rows_here, ends_at):
    return lax.optimization_barrier(jnp.sum((rows_here[:, None] >= ends_at[None, :]).astype(jnp.int32), axis=1))

def token_table(global_rows, request_lens, request_group, prompt_lens):
    ends_at = jnp.cumsum(request_lens)
    starts_at = ends_at - request_lens
    request_of = request_index(global_rows, ends_at)
    one_hot = request_of[:, None] == jnp.arange(request_lens.shape[0], dtype=jnp.int32)[None, :]
    first_row = lax.optimization_barrier(jnp.sum(jnp.where(one_hot, starts_at[None, :], 0), axis=1))
    group_of = lax.optimization_barrier(jnp.sum(jnp.where(one_hot, request_group[None, :], 0), axis=1))
    group_hot = group_of[:, None] == jnp.arange(prompt_lens.shape[0], dtype=jnp.int32)[None, :]
    prefix_of = lax.optimization_barrier(jnp.sum(jnp.where(group_hot, prompt_lens[None, :], 0), axis=1))
    positions = (prefix_of + global_rows - first_row).astype(jnp.float32)
    return (request_of, group_hot, positions, ends_at)

def prompt_mask(prompt_table, prompt_lens, first_block, block_count, block_size):
    blocks = first_block + jnp.arange(block_count, dtype=jnp.int32)
    matching = prompt_table[:, :, None] == blocks[None, None, :]
    present = jnp.any(matching, axis=1)
    slot_no = lax.optimization_barrier(jnp.sum(jnp.where(matching, jnp.arange(prompt_table.shape[1], dtype=jnp.int32)[None, :, None], 0), axis=1))
    within = slot_no[:, :, None] * block_size + jnp.arange(block_size, dtype=jnp.int32)[None, None, :]
    allowed = present[:, :, None] & (within < prompt_lens[:, None, None])
    return allowed.reshape(prompt_table.shape[0], block_count * block_size)

def reference(hidden, norm_gain, query_weight, key_weight, value_weight, query_bias, key_bias, value_bias, request_lens, request_group, prompt_lens, prompt_table, pool_keys, pool_values, prev_cache, dest_device):
    rows_all = jnp.arange(TOKENS, dtype=jnp.int32)
    request_of, group_hot, positions, ends_at = token_table(rows_all, request_lens, request_group, prompt_lens)
    as_float = hidden.astype(jnp.float32)
    inverse = lax.rsqrt(lax.optimization_barrier(jnp.mean(as_float * as_float, axis=1, keepdims=True)) + EPSILON)
    normed = (as_float * inverse * norm_gain.astype(jnp.float32)[None, :]).astype(jnp.bfloat16)
    query_proj = jnp.dot(normed, query_weight, preferred_element_type=jnp.float32) + query_bias.astype(jnp.float32)[None, :]
    key_proj = jnp.dot(normed, key_weight, preferred_element_type=jnp.float32) + key_bias.astype(jnp.float32)[None, :]
    value_proj = jnp.dot(normed, value_weight, preferred_element_type=jnp.float32) + value_bias.astype(jnp.float32)[None, :]
    queries = rotary(query_proj.reshape(TOKENS, QH, HD), positions).astype(jnp.bfloat16)
    keys_new = rotary(key_proj.reshape(TOKENS, KV, HD), positions).astype(jnp.bfloat16)
    values_new = value_proj.astype(jnp.bfloat16).reshape(TOKENS, KV, HD)
    allowed_group = prompt_mask(prompt_table, prompt_lens, 0, POOL_BLK, BS)
    prompt_allowed = jnp.any(group_hot[:, :, None] & allowed_group[None, :, :], axis=1)
    span_allowed = (request_of[:, None] == request_of[None, :]) & (rows_all[None, :] <= rows_all[:, None])
    allowed = jnp.concatenate([prompt_allowed, span_allowed], axis=1)
    all_keys = jnp.concatenate([pool_keys.reshape(POOL_BLK * BS, KV, HD), keys_new], axis=0)
    all_values = jnp.concatenate([pool_values.reshape(POOL_BLK * BS, KV, HD), values_new], axis=0)
    group_size = QH // KV
    score_scale = HD ** (-0.5)

    def one_head(head_no):
        query_head = lax.dynamic_index_in_dim(queries, head_no, axis=1, keepdims=False)
        key_head = lax.dynamic_index_in_dim(all_keys, head_no // group_size, axis=1, keepdims=False)
        value_head = lax.dynamic_index_in_dim(all_values, head_no // group_size, axis=1, keepdims=False)
        scores = jnp.dot(query_head, key_head.T, preferred_element_type=jnp.float32) * score_scale
        scores = jnp.where(allowed, scores, NEG_BIG)
        row_max = lax.optimization_barrier(jnp.max(scores, axis=1, keepdims=True))
        weights = jnp.where(allowed, jnp.exp(scores - row_max), 0.0)
        row_sum = lax.optimization_barrier(jnp.sum(weights, axis=1, keepdims=True))
        weighted = jnp.dot(weights.astype(jnp.bfloat16), value_head, preferred_element_type=jnp.float32)
        return weighted / row_sum
    heads_out = lax.map(one_head, jnp.arange(QH, dtype=jnp.int32))
    context = jnp.transpose(heads_out, (1, 0, 2)).reshape(TOKENS, QH * HD).astype(jnp.bfloat16)
    target = dest_device[:, 0]
    hit_table = (target[:, None] == jnp.arange(N_DP, dtype=jnp.int32)[None, :]).astype(jnp.int32)
    before = jnp.cumsum(hit_table, axis=0) - hit_table
    block_rank = lax.optimization_barrier(jnp.sum(before * hit_table, axis=1))
    slot_index = (target * BLK_DEV + block_rank).astype(jnp.int32)
    decode_cache = jnp.zeros_like(prev_cache).at[slot_index].set(prev_cache)
    return (context, decode_cache)
```

```python
import math

import jax
import jax.numpy as jnp
from jax import lax
from jax.sharding import Mesh, PartitionSpec as P

HD = 128
CAP = 2
MAX_REQUEST = 3072


NEG_BIG = -1e30
EPSILON = 1e-06
THETA = 1000000.0


def rotary(values, positions):
    head_dim = values.shape[-1]
    half_dim = head_dim // 2
    frequency = jnp.exp(
        -jnp.arange(half_dim, dtype=jnp.float32) * (2.0 / head_dim) * math.log(THETA)
    )
    angles = positions[:, None] * frequency[None, :]
    cosine = jnp.concatenate([jnp.cos(angles), jnp.cos(angles)], axis=-1)[:, None, :]
    sine_part = jnp.concatenate([jnp.sin(angles), jnp.sin(angles)], axis=-1)[:, None, :]
    first_half = values[..., :half_dim]
    second_half = values[..., half_dim:]
    turned = jnp.concatenate([-second_half, first_half], axis=-1)
    return values * cosine + turned * sine_part


def request_index(rows_here, ends_at):
    return jnp.sum((rows_here[:, None] >= ends_at[None, :]).astype(jnp.int32), axis=1)


def token_table(global_rows, request_lens, request_group, prompt_lens):
    ends_at = jnp.cumsum(request_lens)
    starts_at = ends_at - request_lens
    request_of = request_index(global_rows, ends_at)
    one_hot = request_of[:, None] == jnp.arange(request_lens.shape[0], dtype=jnp.int32)[None, :]
    first_row = jnp.sum(jnp.where(one_hot, starts_at[None, :], 0), axis=1)
    group_of = jnp.sum(jnp.where(one_hot, request_group[None, :], 0), axis=1)
    group_hot = group_of[:, None] == jnp.arange(prompt_lens.shape[0], dtype=jnp.int32)[None, :]
    prefix_of = jnp.sum(jnp.where(group_hot, prompt_lens[None, :], 0), axis=1)
    positions = (prefix_of + global_rows - first_row).astype(jnp.float32)
    return (request_of, group_hot, positions, ends_at)


def prompt_mask(prompt_table, prompt_lens, block_count, block_size):
    blocks = jnp.arange(block_count, dtype=jnp.int32)
    matching = prompt_table[:, :, None] == blocks[None, None, :]
    present = jnp.any(matching, axis=1)
    slot_no = jnp.sum(
        jnp.where(matching, jnp.arange(prompt_table.shape[1], dtype=jnp.int32)[None, :, None], 0),
        axis=1,
    )
    within = (
        slot_no[:, :, None] * block_size + jnp.arange(block_size, dtype=jnp.int32)[None, None, :]
    )
    allowed = present[:, :, None] & (within < prompt_lens[:, None, None])
    return allowed.reshape(prompt_table.shape[0], block_count * block_size)


def attend(current, queries, keys_flat, values_flat, allowed, score_scale):
    best_score, total_sum, accumulated = current
    scores = (
        jnp.einsum("kgqd,skd->kgqs", queries, keys_flat, preferred_element_type=jnp.float32)
        * score_scale
    )
    masked = allowed[None, None, :, :]
    scores = jnp.where(masked, scores, NEG_BIG)
    new_best = jnp.maximum(best_score, jnp.max(scores, axis=-1))
    weights = jnp.where(masked, jnp.exp(scores - new_best[..., None]), 0.0)
    factor = jnp.exp(best_score - new_best)
    total_sum = total_sum * factor + jnp.sum(weights, axis=-1)
    accumulated = accumulated * factor[..., None] + jnp.einsum(
        "kgqs,skd->kgqd",
        weights.astype(jnp.bfloat16),
        values_flat,
        preferred_element_type=jnp.float32,
    )
    return (new_best, total_sum, accumulated)


def dp_index():
    return lax.axis_index("dz") * lax.axis_size("dc") + lax.axis_index("dc")


def relayout(prev_cache, dest_device):
    blocks_here = prev_cache.shape[0]
    devices = lax.axis_size("dz") * lax.axis_size("dc")
    slot_count = devices * CAP
    target = dest_device[:, 0]
    same_target = target[:, None] == target[None, :]
    earlier = (
        jnp.arange(blocks_here, dtype=jnp.int32)[None, :]
        < jnp.arange(blocks_here, dtype=jnp.int32)[:, None]
    )
    block_rank = jnp.sum((same_target & earlier).astype(jnp.int32), axis=1)
    slot_device = jnp.arange(slot_count, dtype=jnp.int32) // CAP
    slot_rank = jnp.arange(slot_count, dtype=jnp.int32) % CAP
    matches = (target[None, :] == slot_device[:, None]) & (
        block_rank[None, :] == slot_rank[:, None]
    )
    filled = jnp.any(matches, axis=1)
    source = jnp.sum(
        jnp.where(matches, jnp.arange(blocks_here, dtype=jnp.int32)[None, :], 0), axis=1
    )
    packed = jnp.take(prev_cache, source, axis=0)
    packed = jnp.where(filled[:, None, None, None, None], packed, jnp.zeros_like(packed))
    slot_flags = filled.astype(jnp.bfloat16)
    arrived, arrived_flags = (
        lax.all_to_all(packed, ("dz", "dc"), split_axis=0, concat_axis=0, tiled=True),
        lax.all_to_all(slot_flags, ("dz", "dc"), split_axis=0, concat_axis=0, tiled=True),
    )
    arrived_live = arrived_flags > 0.5
    order_no = jnp.cumsum(arrived_live.astype(jnp.int32)) - 1
    picked = arrived_live[None, :] & (
        order_no[None, :] == jnp.arange(blocks_here, dtype=jnp.int32)[:, None]
    )
    chosen = jnp.sum(jnp.where(picked, jnp.arange(slot_count, dtype=jnp.int32)[None, :], 0), axis=1)
    return jnp.take(arrived, chosen, axis=0)


def per_device(
    hidden,
    norm_gain,
    query_weight,
    key_weight,
    value_weight,
    query_bias,
    key_bias,
    value_bias,
    request_lens,
    request_group,
    prompt_lens,
    prompt_table,
    pool_keys,
    pool_values,
    prev_cache,
    dest_device,
):
    decode_cache = relayout(prev_cache, dest_device)
    row_count = hidden.shape[0]
    me = dp_index()
    side = lax.axis_index("dc")
    sides = lax.axis_size("dc")
    global_rows = me * row_count + jnp.arange(row_count, dtype=jnp.int32)
    request_of, group_hot, positions, ends_at = token_table(
        global_rows, request_lens, request_group, prompt_lens
    )
    full_rows = lax.all_gather(hidden, "mp", axis=1, tiled=True)
    q_cols = query_weight.shape[1]
    k_cols = key_weight.shape[1]
    weights_here = jnp.concatenate([query_weight, key_weight, value_weight], axis=1)
    weights_mine = lax.all_gather(weights_here, "dz", axis=0, tiled=True)
    weights_other = lax.ppermute(weights_mine, "dc", perm=[(0, 1), (1, 0)])
    pool_here = jnp.concatenate([pool_keys, pool_values], axis=2)
    pool_all = lax.all_gather(pool_here, ("dz", "dc"), axis=0, tiled=True)
    as_float = full_rows.astype(jnp.float32)
    inverse = lax.rsqrt(jnp.mean(as_float * as_float, axis=1, keepdims=True) + EPSILON)
    normed = (as_float * inverse * norm_gain.astype(jnp.float32)[None, :]).astype(jnp.bfloat16)
    block_rows = weights_here.shape[0]
    split = normed.reshape(row_count, -1, sides, block_rows)
    normed_mine = lax.dynamic_index_in_dim(split, side, axis=2, keepdims=False)
    normed_other = lax.dynamic_index_in_dim(split, sides - 1 - side, axis=2, keepdims=False)
    proj = jnp.dot(
        normed_mine.reshape(row_count, -1), weights_mine, preferred_element_type=jnp.float32
    ) + jnp.dot(
        normed_other.reshape(row_count, -1), weights_other, preferred_element_type=jnp.float32
    )
    query_proj = proj[:, :q_cols] + query_bias.astype(jnp.float32)[None, :]
    key_proj = proj[:, q_cols:q_cols + k_cols] + key_bias.astype(jnp.float32)[None, :]
    value_proj = proj[:, q_cols + k_cols:] + value_bias.astype(jnp.float32)[None, :]
    local_heads = query_proj.shape[1] // HD
    local_kv = key_proj.shape[1] // HD
    group_size = local_heads // local_kv
    queries = rotary(query_proj.reshape(row_count, local_heads, HD), positions).astype(jnp.bfloat16)
    queries = queries.reshape(row_count, local_kv, group_size, HD).transpose(1, 2, 0, 3)
    keys_new = (
        rotary(key_proj.reshape(row_count, local_kv, HD), positions)
        .astype(jnp.bfloat16)
        .reshape(row_count, local_kv * HD)
    )
    values_new = value_proj.astype(jnp.bfloat16)
    span_here = jnp.concatenate([keys_new, values_new], axis=1)
    span_all = lax.all_gather(span_here, ("dz", "dc"), axis=0, tiled=True)
    score_scale = HD ** (-0.5)
    carried = (
        jnp.full((local_kv, group_size, row_count), NEG_BIG, jnp.float32),
        jnp.zeros((local_kv, group_size, row_count), jnp.float32),
        jnp.zeros((local_kv, group_size, row_count, HD), jnp.float32),
    )
    block_size = pool_all.shape[1]
    blocks_here = pool_all.shape[0]
    kv_width = local_kv * HD
    allowed_group = prompt_mask(prompt_table, prompt_lens, blocks_here, block_size)
    allowed = jnp.any(group_hot[:, :, None] & allowed_group[None, :, :], axis=1)
    keys_flat = pool_all[:, :, :kv_width].reshape(blocks_here * block_size, local_kv, HD)
    values_flat = pool_all[:, :, kv_width:].reshape(blocks_here * block_size, local_kv, HD)
    carried = attend(carried, queries, keys_flat, values_flat, allowed, score_scale)
    key_count = span_all.shape[0]
    window = min(key_count, MAX_REQUEST + row_count)
    window = -(-window // row_count) * row_count
    window_start = jnp.maximum((me + 1) * row_count - window, 0)
    span_window = lax.dynamic_slice_in_dim(span_all, window_start, window, axis=0)
    key_rows = window_start + jnp.arange(window, dtype=jnp.int32)
    key_request = request_index(key_rows, ends_at)
    span_allowed = (request_of[:, None] == key_request[None, :]) & (
        key_rows[None, :] <= global_rows[:, None]
    )
    span_keys_flat = span_window[:, :kv_width].reshape(window, local_kv, HD)
    span_values_flat = span_window[:, kv_width:].reshape(window, local_kv, HD)
    carried = attend(
        carried, queries, span_keys_flat, span_values_flat, span_allowed, score_scale
    )
    best_score, total_sum, accumulated = carried
    output = accumulated / total_sum[..., None]
    context = output.transpose(2, 0, 1, 3).reshape(row_count, local_heads * HD).astype(jnp.bfloat16)
    return (context, decode_cache)


def solution(mesh):
    dp_size, mp_size = mesh.devices.shape
    inner = Mesh(mesh.devices.reshape(dp_size // 2, 2, mp_size), ("dz", "dc", "mp"))
    dp = ("dz", "dc")
    return jax.shard_map(
        per_device,
        mesh=inner,
        in_specs=(
            P(dp, "mp"),
            P(),
            P(dp, "mp"),
            P(dp, "mp"),
            P(dp, "mp"),
            P("mp"),
            P("mp"),
            P("mp"),
            P(),
            P(),
            P(),
            P(),
            P(dp, None, "mp"),
            P(dp, None, "mp"),
            P(dp, None, None, None, "mp"),
            P(dp, None),
        ),
        out_specs=(P(dp, "mp"), P(dp, None, None, None, "mp")),
        check_vma=False,
    )
```

```python
import math

import jax
import jax.numpy as jnp
from jax import lax
from jax.sharding import Mesh, PartitionSpec as P

HD = 128
CAP = 2
MAX_REQUEST = 3072


NEG_BIG = -1e30
EPSILON = 1e-06
THETA = 1000000.0


def rotary(values, positions):
    head_dim = values.shape[-1]
    half_dim = head_dim // 2
    frequency = jnp.exp(
        -jnp.arange(half_dim, dtype=jnp.float32) * (2.0 / head_dim) * math.log(THETA)
    )
    angles = positions[:, None] * frequency[None, :]
    cosine = jnp.concatenate([jnp.cos(angles), jnp.cos(angles)], axis=-1)[:, None, :]
    sine_part = jnp.concatenate([jnp.sin(angles), jnp.sin(angles)], axis=-1)[:, None, :]
    first_half = values[..., :half_dim]
    second_half = values[..., half_dim:]
    turned = jnp.concatenate([-second_half, first_half], axis=-1)
    return values * cosine + turned * sine_part


def request_index(rows_here, ends_at):
    return jnp.sum((rows_here[:, None] >= ends_at[None, :]).astype(jnp.int32), axis=1)


def token_table(global_rows, request_lens, request_group, prompt_lens):
    ends_at = jnp.cumsum(request_lens)
    starts_at = ends_at - request_lens
    request_of = request_index(global_rows, ends_at)
    one_hot = request_of[:, None] == jnp.arange(request_lens.shape[0], dtype=jnp.int32)[None, :]
    first_row = jnp.sum(jnp.where(one_hot, starts_at[None, :], 0), axis=1)
    group_of = jnp.sum(jnp.where(one_hot, request_group[None, :], 0), axis=1)
    group_hot = group_of[:, None] == jnp.arange(prompt_lens.shape[0], dtype=jnp.int32)[None, :]
    prefix_of = jnp.sum(jnp.where(group_hot, prompt_lens[None, :], 0), axis=1)
    positions = (prefix_of + global_rows - first_row).astype(jnp.float32)
    return (request_of, group_hot, positions, ends_at)


def prompt_mask(prompt_table, prompt_lens, block_count, block_size):
    blocks = jnp.arange(block_count, dtype=jnp.int32)
    matching = prompt_table[:, :, None] == blocks[None, None, :]
    present = jnp.any(matching, axis=1)
    slot_no = jnp.sum(
        jnp.where(matching, jnp.arange(prompt_table.shape[1], dtype=jnp.int32)[None, :, None], 0),
        axis=1,
    )
    within = (
        slot_no[:, :, None] * block_size + jnp.arange(block_size, dtype=jnp.int32)[None, None, :]
    )
    allowed = present[:, :, None] & (within < prompt_lens[:, None, None])
    return allowed.reshape(prompt_table.shape[0], block_count * block_size)


def attend(current, queries, keys_flat, values_flat, allowed, score_scale):
    best_score, total_sum, accumulated = current
    scores = (
        jnp.einsum("kgqd,skd->kgqs", queries, keys_flat, preferred_element_type=jnp.float32)
        * score_scale
    )
    masked = allowed[None, None, :, :]
    scores = jnp.where(masked, scores, NEG_BIG)
    new_best = jnp.maximum(best_score, jnp.max(scores, axis=-1))
    weights = jnp.where(masked, jnp.exp(scores - new_best[..., None]), 0.0)
    factor = jnp.exp(best_score - new_best)
    total_sum = total_sum * factor + jnp.sum(weights, axis=-1)
    accumulated = accumulated * factor[..., None] + jnp.einsum(
        "kgqs,skd->kgqd",
        weights.astype(jnp.bfloat16),
        values_flat,
        preferred_element_type=jnp.float32,
    )
    return (new_best, total_sum, accumulated)


def dp_index():
    return lax.axis_index("dz") * lax.axis_size("dc") + lax.axis_index("dc")


def relayout(prev_cache, dest_device):
    blocks_here = prev_cache.shape[0]
    devices = lax.axis_size("dz") * lax.axis_size("dc")
    slot_count = devices * CAP
    target = dest_device[:, 0]
    same_target = target[:, None] == target[None, :]
    earlier = (
        jnp.arange(blocks_here, dtype=jnp.int32)[None, :]
        < jnp.arange(blocks_here, dtype=jnp.int32)[:, None]
    )
    block_rank = jnp.sum((same_target & earlier).astype(jnp.int32), axis=1)
    slot_device = jnp.arange(slot_count, dtype=jnp.int32) // CAP
    slot_rank = jnp.arange(slot_count, dtype=jnp.int32) % CAP
    matches = (target[None, :] == slot_device[:, None]) & (
        block_rank[None, :] == slot_rank[:, None]
    )
    filled = jnp.any(matches, axis=1)
    source = jnp.sum(
        jnp.where(matches, jnp.arange(blocks_here, dtype=jnp.int32)[None, :], 0), axis=1
    )
    packed = jnp.take(prev_cache, source, axis=0)
    slot_flags = filled.astype(jnp.bfloat16)
    arrived, arrived_flags = (
        lax.all_to_all(packed, ("dz", "dc"), split_axis=0, concat_axis=0, tiled=True),
        lax.all_to_all(slot_flags, ("dz", "dc"), split_axis=0, concat_axis=0, tiled=True),
    )
    arrived_live = arrived_flags > 0.5
    order_no = jnp.cumsum(arrived_live.astype(jnp.int32)) - 1
    picked = arrived_live[None, :] & (
        order_no[None, :] == jnp.arange(blocks_here, dtype=jnp.int32)[:, None]
    )
    chosen = jnp.sum(jnp.where(picked, jnp.arange(slot_count, dtype=jnp.int32)[None, :], 0), axis=1)
    return jnp.take(arrived, chosen, axis=0)


def per_device(
    hidden,
    norm_gain,
    query_weight,
    key_weight,
    value_weight,
    query_bias,
    key_bias,
    value_bias,
    request_lens,
    request_group,
    prompt_lens,
    prompt_table,
    pool_keys,
    pool_values,
    prev_cache,
    dest_device,
):
    row_count = hidden.shape[0]
    me = dp_index()
    side = lax.axis_index("dc")
    sides = lax.axis_size("dc")
    global_rows = me * row_count + jnp.arange(row_count, dtype=jnp.int32)
    request_of, group_hot, positions, ends_at = token_table(
        global_rows, request_lens, request_group, prompt_lens
    )
    mp_size = lax.axis_size("mp")
    spread = jnp.broadcast_to(hidden[None], (mp_size,) + hidden.shape)
    pieces = lax.all_to_all(spread, "mp", split_axis=0, concat_axis=0, tiled=True)
    q_cols = query_weight.shape[1]
    k_cols = key_weight.shape[1]
    block_rows = query_weight.shape[0]
    pool_here = jnp.concatenate([pool_keys, pool_values], axis=2).reshape(block_rows, -1)
    weights_here = jnp.concatenate([query_weight, key_weight, value_weight, pool_here], axis=1)
    weights_all = lax.all_gather(weights_here, ("dz", "dc"), axis=0, tiled=True)
    proj_cols = q_cols + 2 * k_cols
    pool_all = weights_all[:, proj_cols:].reshape(
        (-1,) + pool_keys.shape[1:2] + (2 * pool_keys.shape[2],)
    )
    as_float = pieces.astype(jnp.float32)
    inverse = lax.rsqrt(
        jnp.mean(jnp.sum(as_float * as_float, axis=2), axis=0)[None, :, None] / pieces.shape[2]
        + EPSILON
    )
    gain = norm_gain.astype(jnp.float32).reshape(mp_size, 1, -1)
    normed = (as_float * inverse * gain).astype(jnp.bfloat16)
    proj = jnp.einsum(
        "jtf,jfc->tc",
        normed,
        weights_all.reshape(mp_size, -1, weights_all.shape[1]),
        preferred_element_type=jnp.float32,
    )
    query_proj = proj[:, :q_cols] + query_bias.astype(jnp.float32)[None, :]
    key_proj = proj[:, q_cols:q_cols + k_cols] + key_bias.astype(jnp.float32)[None, :]
    value_proj = proj[:, q_cols + k_cols:proj_cols] + value_bias.astype(jnp.float32)[None, :]
    local_heads = query_proj.shape[1] // HD
    local_kv = key_proj.shape[1] // HD
    group_size = local_heads // local_kv
    queries = rotary(query_proj.reshape(row_count, local_heads, HD), positions).astype(jnp.bfloat16)
    queries = queries.reshape(row_count, local_kv, group_size, HD).transpose(1, 2, 0, 3)
    keys_new = (
        rotary(key_proj.reshape(row_count, local_kv, HD), positions)
        .astype(jnp.bfloat16)
        .reshape(row_count, local_kv * HD)
    )
    values_new = value_proj.astype(jnp.bfloat16)
    span_here = jnp.concatenate([keys_new, values_new], axis=1)
    span_all = lax.all_gather(span_here, ("dz", "dc"), axis=0, tiled=True)
    prev_cache, span_all = lax.optimization_barrier((prev_cache, span_all))
    decode_cache = relayout(prev_cache, dest_device)
    score_scale = HD ** (-0.5)
    carried = (
        jnp.full((local_kv, group_size, row_count), NEG_BIG, jnp.float32),
        jnp.zeros((local_kv, group_size, row_count), jnp.float32),
        jnp.zeros((local_kv, group_size, row_count, HD), jnp.float32),
    )
    block_size = pool_all.shape[1]
    blocks_here = pool_all.shape[0]
    kv_width = local_kv * HD
    allowed_group = prompt_mask(prompt_table, prompt_lens, blocks_here, block_size)
    allowed = jnp.any(group_hot[:, :, None] & allowed_group[None, :, :], axis=1)
    keys_flat = pool_all[:, :, :kv_width].reshape(blocks_here * block_size, local_kv, HD)
    values_flat = pool_all[:, :, kv_width:].reshape(blocks_here * block_size, local_kv, HD)
    carried = attend(carried, queries, keys_flat, values_flat, allowed, score_scale)
    key_count = span_all.shape[0]
    window = min(key_count, MAX_REQUEST + row_count)
    window = -(-window // row_count) * row_count
    window_start = jnp.maximum((me + 1) * row_count - window, 0)
    span_window = lax.dynamic_slice_in_dim(span_all, window_start, window, axis=0)
    key_rows = window_start + jnp.arange(window, dtype=jnp.int32)
    key_request = request_index(key_rows, ends_at)
    span_allowed = (request_of[:, None] == key_request[None, :]) & (
        key_rows[None, :] <= global_rows[:, None]
    )
    span_keys_flat = span_window[:, :kv_width].reshape(window, local_kv, HD)
    span_values_flat = span_window[:, kv_width:].reshape(window, local_kv, HD)
    carried = attend(
        carried, queries, span_keys_flat, span_values_flat, span_allowed, score_scale
    )
    best_score, total_sum, accumulated = carried
    output = accumulated / total_sum[..., None]
    context = output.transpose(2, 0, 1, 3).reshape(row_count, local_heads * HD).astype(jnp.bfloat16)
    return (context, decode_cache)


def solution(mesh):
    dp_size, mp_size = mesh.devices.shape
    inner = Mesh(mesh.devices.reshape(dp_size // 2, 2, mp_size), ("dz", "dc", "mp"))
    dp = ("dz", "dc")
    return jax.shard_map(
        per_device,
        mesh=inner,
        in_specs=(
            P(dp, "mp"),
            P(),
            P(dp, "mp"),
            P(dp, "mp"),
            P(dp, "mp"),
            P("mp"),
            P("mp"),
            P("mp"),
            P(),
            P(),
            P(),
            P(),
            P(dp, None, "mp"),
            P(dp, None, "mp"),
            P(dp, None, None, None, "mp"),
            P(dp, None),
        ),
        out_specs=(P(dp, "mp"), P(dp, None, None, None, "mp")),
        check_vma=False,
    )
```

```python
import math

import jax
import jax.numpy as jnp
from jax import lax
from jax.sharding import Mesh, PartitionSpec as P


HD = 128
CAP = 2
MAX_REQUEST = 3072


NEG_BIG = -1e30
EPSILON = 1e-06
THETA = 1000000.0


def rotary(values, positions):
    head_dim = values.shape[-1]
    half_dim = head_dim // 2
    frequency = jnp.exp(
        -jnp.arange(half_dim, dtype=jnp.float32) * (2.0 / head_dim) * math.log(THETA)
    )
    angles = positions[:, None] * frequency[None, :]
    cosine = jnp.concatenate([jnp.cos(angles), jnp.cos(angles)], axis=-1)[:, None, :]
    sine_part = jnp.concatenate([jnp.sin(angles), jnp.sin(angles)], axis=-1)[:, None, :]
    first_half = values[..., :half_dim]
    second_half = values[..., half_dim:]
    turned = jnp.concatenate([-second_half, first_half], axis=-1)
    return values * cosine + turned * sine_part


def request_index(rows_here, ends_at):
    return jnp.sum((rows_here[:, None] >= ends_at[None, :]).astype(jnp.int32), axis=1)


def token_table(global_rows, request_lens, request_group, prompt_lens):
    ends_at = jnp.cumsum(request_lens)
    starts_at = ends_at - request_lens
    request_of = request_index(global_rows, ends_at)
    one_hot = request_of[:, None] == jnp.arange(request_lens.shape[0], dtype=jnp.int32)[None, :]
    first_row = jnp.sum(jnp.where(one_hot, starts_at[None, :], 0), axis=1)
    group_of = jnp.sum(jnp.where(one_hot, request_group[None, :], 0), axis=1)
    group_hot = group_of[:, None] == jnp.arange(prompt_lens.shape[0], dtype=jnp.int32)[None, :]
    prefix_of = jnp.sum(jnp.where(group_hot, prompt_lens[None, :], 0), axis=1)
    positions = (prefix_of + global_rows - first_row).astype(jnp.float32)
    return (request_of, group_hot, positions, ends_at)


def prompt_mask(prompt_table, prompt_lens, blocks, block_size):
    block_count = blocks.shape[0]
    matching = prompt_table[:, :, None] == blocks[None, None, :]
    present = jnp.any(matching, axis=1)
    slot_no = jnp.sum(
        jnp.where(matching, jnp.arange(prompt_table.shape[1], dtype=jnp.int32)[None, :, None], 0),
        axis=1,
    )
    within = (
        slot_no[:, :, None] * block_size + jnp.arange(block_size, dtype=jnp.int32)[None, None, :]
    )
    allowed = present[:, :, None] & (within < prompt_lens[:, None, None])
    return allowed.reshape(prompt_table.shape[0], block_count * block_size)


def attend(current, queries, keys_flat, values_flat, allowed, score_scale):
    best_score, total_sum, accumulated = current
    scores = (
        jnp.einsum("kgqd,skd->kgqs", queries, keys_flat, preferred_element_type=jnp.float32)
        * score_scale
    )
    masked = allowed[None, None, :, :]
    scores = jnp.where(masked, scores, NEG_BIG)
    new_best = jnp.maximum(best_score, jnp.max(scores, axis=-1))
    weights = jnp.where(masked, jnp.exp(scores - new_best[..., None]), 0.0)
    factor = jnp.exp(best_score - new_best)
    total_sum = total_sum * factor + jnp.sum(weights, axis=-1)
    accumulated = accumulated * factor[..., None] + jnp.einsum(
        "kgqs,skd->kgqd",
        weights.astype(jnp.bfloat16),
        values_flat,
        preferred_element_type=jnp.float32,
    )
    return (new_best, total_sum, accumulated)


def dp_index():
    return lax.axis_index("dz") * lax.axis_size("dc") + lax.axis_index("dc")


def relayout(prev_cache, dest_device):
    blocks_here = prev_cache.shape[0]
    devices = lax.axis_size("dz") * lax.axis_size("dc")
    slot_count = devices * CAP
    target = dest_device[:, 0]
    same_target = target[:, None] == target[None, :]
    earlier = (
        jnp.arange(blocks_here, dtype=jnp.int32)[None, :]
        < jnp.arange(blocks_here, dtype=jnp.int32)[:, None]
    )
    block_rank = jnp.sum((same_target & earlier).astype(jnp.int32), axis=1)
    slot_device = jnp.arange(slot_count, dtype=jnp.int32) // CAP
    slot_rank = jnp.arange(slot_count, dtype=jnp.int32) % CAP
    matches = (target[None, :] == slot_device[:, None]) & (
        block_rank[None, :] == slot_rank[:, None]
    )
    filled = jnp.any(matches, axis=1)
    source = jnp.sum(
        jnp.where(matches, jnp.arange(blocks_here, dtype=jnp.int32)[None, :], 0), axis=1
    )
    packed = jnp.take(prev_cache, source, axis=0)
    slot_flags = filled.astype(jnp.bfloat16)
    arrived, arrived_flags = (
        lax.all_to_all(packed, ("dz", "dc"), split_axis=0, concat_axis=0, tiled=True),
        lax.all_to_all(slot_flags, ("dz", "dc"), split_axis=0, concat_axis=0, tiled=True),
    )
    arrived_live = arrived_flags > 0.5
    order_no = jnp.cumsum(arrived_live.astype(jnp.int32)) - 1
    picked = arrived_live[None, :] & (
        order_no[None, :] == jnp.arange(blocks_here, dtype=jnp.int32)[:, None]
    )
    chosen = jnp.sum(jnp.where(picked, jnp.arange(slot_count, dtype=jnp.int32)[None, :], 0), axis=1)
    return jnp.take(arrived, chosen, axis=0)


def layer(
    hidden,
    norm_gain,
    query_weight,
    key_weight,
    value_weight,
    query_bias,
    key_bias,
    value_bias,
    request_lens,
    request_group,
    prompt_lens,
    prompt_table,
    pool_keys,
    pool_values,
    prev_cache,
    dest_device,
):
    row_count = hidden.shape[0]
    me = dp_index()
    global_rows = me * row_count + jnp.arange(row_count, dtype=jnp.int32)
    request_of, group_hot, positions, ends_at = token_table(
        global_rows, request_lens, request_group, prompt_lens
    )
    mp_size = lax.axis_size("mp")
    spread = jnp.broadcast_to(hidden[None], (mp_size,) + hidden.shape)
    pieces = lax.all_to_all(spread, "mp", split_axis=0, concat_axis=0, tiled=True)
    q_cols = query_weight.shape[1]
    k_cols = key_weight.shape[1]
    block_rows = query_weight.shape[0]
    pool_here = jnp.concatenate([pool_keys, pool_values], axis=2).reshape(block_rows, -1)
    weights_here = jnp.concatenate([query_weight, key_weight, value_weight, pool_here], axis=1)
    proj_cols = q_cols + 2 * k_cols
    me16 = me
    nd = lax.axis_size("dz") * lax.axis_size("dc")
    dp_axes = ("dz", "dc")

    def shift(x, pairs):
        return lax.ppermute(x, dp_axes, perm=pairs)

    y_swap = [(p, p ^ 2) for p in range(nd)]
    z_up = [(p, (p + 4) % nd) for p in range(nd)]
    z_down = [(p, (p - 4) % nd) for p in range(nd)]
    half_rows = block_rows // 2
    wave_a = weights_here
    wave_b = shift(wave_a, y_swap)
    held = []
    for wave in (wave_a, wave_b):
        from_below = shift(wave, z_up)
        from_above = shift(wave, z_down)
        far_low = shift(from_below[:half_rows], z_up)
        far_high = shift(from_above[half_rows:], z_down)
        held.extend([wave, from_below, from_above, jnp.concatenate([far_low, far_high], axis=0)])
    ids_a = [me16, (me16 - 4) % nd, (me16 + 4) % nd, (me16 + 8) % nd]
    ids = jnp.stack(ids_a + [i ^ 2 for i in ids_a])
    weights_mine = jnp.concatenate(held[0:4] + held[4:8], axis=0)
    weights_other = shift(weights_mine, [(p, p ^ 1) for p in range(nd)])
    ids_other = ids ^ 1
    block_ids = jnp.concatenate([ids, ids_other])
    pool_rows = jnp.concatenate([weights_mine[:, proj_cols:], weights_other[:, proj_cols:]], axis=0)
    pool_all = pool_rows.reshape((-1,) + pool_keys.shape[1:2] + (2 * pool_keys.shape[2],))
    as_float = pieces.astype(jnp.float32)
    inverse = lax.rsqrt(
        jnp.mean(jnp.sum(as_float * as_float, axis=2), axis=0)[None, :, None] / pieces.shape[2]
        + EPSILON
    )
    gain = norm_gain.astype(jnp.float32).reshape(mp_size, 1, -1)
    normed = (as_float * inverse * gain).astype(jnp.bfloat16)
    per_piece = pieces.shape[2] // block_rows
    normed_blocks = normed.reshape(mp_size, row_count, per_piece, block_rows)
    normed_blocks = normed_blocks.transpose(0, 2, 1, 3).reshape(-1, row_count, block_rows)

    def pick(which):
        chosen = jnp.take(normed_blocks, which, axis=0)
        return chosen.transpose(1, 0, 2).reshape(row_count, -1)

    proj = jnp.dot(pick(ids), weights_mine, preferred_element_type=jnp.float32) + jnp.dot(
        pick(ids_other), weights_other, preferred_element_type=jnp.float32
    )
    query_proj = proj[:, :q_cols] + query_bias.astype(jnp.float32)[None, :]
    key_proj = proj[:, q_cols:q_cols + k_cols] + key_bias.astype(jnp.float32)[None, :]
    value_proj = proj[:, q_cols + k_cols:proj_cols] + value_bias.astype(jnp.float32)[None, :]
    local_heads = query_proj.shape[1] // HD
    local_kv = key_proj.shape[1] // HD
    group_size = local_heads // local_kv
    queries = rotary(query_proj.reshape(row_count, local_heads, HD), positions).astype(jnp.bfloat16)
    queries = queries.reshape(row_count, local_kv, group_size, HD).transpose(1, 2, 0, 3)
    keys_new = (
        rotary(key_proj.reshape(row_count, local_kv, HD), positions)
        .astype(jnp.bfloat16)
        .reshape(row_count, local_kv * HD)
    )
    values_new = value_proj.astype(jnp.bfloat16)
    span_here = jnp.concatenate([keys_new, values_new], axis=1)
    span_all = lax.all_gather(span_here, ("dz", "dc"), axis=0, tiled=True)
    prev_cache, span_all = lax.optimization_barrier((prev_cache, span_all))
    decode_cache = relayout(prev_cache, dest_device)
    score_scale = HD ** (-0.5)
    carried = (
        jnp.full((local_kv, group_size, row_count), NEG_BIG, jnp.float32),
        jnp.zeros((local_kv, group_size, row_count), jnp.float32),
        jnp.zeros((local_kv, group_size, row_count, HD), jnp.float32),
    )
    block_size = pool_all.shape[1]
    blocks_here = pool_all.shape[0]
    kv_width = local_kv * HD
    allowed_group = prompt_mask(prompt_table, prompt_lens, block_ids, block_size)
    allowed = jnp.any(group_hot[:, :, None] & allowed_group[None, :, :], axis=1)
    keys_flat = pool_all[:, :, :kv_width].reshape(blocks_here * block_size, local_kv, HD)
    values_flat = pool_all[:, :, kv_width:].reshape(blocks_here * block_size, local_kv, HD)
    carried = attend(carried, queries, keys_flat, values_flat, allowed, score_scale)
    key_count = span_all.shape[0]
    window = min(key_count, MAX_REQUEST + row_count)
    window = -(-window // row_count) * row_count
    window_start = jnp.maximum((me + 1) * row_count - window, 0)
    span_window = lax.dynamic_slice_in_dim(span_all, window_start, window, axis=0)
    key_rows = window_start + jnp.arange(window, dtype=jnp.int32)
    key_request = request_index(key_rows, ends_at)
    span_allowed = (request_of[:, None] == key_request[None, :]) & (
        key_rows[None, :] <= global_rows[:, None]
    )
    span_keys_flat = span_window[:, :kv_width].reshape(window, local_kv, HD)
    span_values_flat = span_window[:, kv_width:].reshape(window, local_kv, HD)
    carried = attend(
        carried, queries, span_keys_flat, span_values_flat, span_allowed, score_scale
    )
    _, total_sum, accumulated = carried
    output = accumulated / total_sum[..., None]
    context = output.transpose(2, 0, 1, 3).reshape(row_count, local_heads * HD).astype(jnp.bfloat16)
    return (context, decode_cache)


def solution(mesh):
    dp_size, mp_size = mesh.devices.shape
    inner = Mesh(mesh.devices.reshape(dp_size // 2, 2, mp_size), ("dz", "dc", "mp"))
    dp = ("dz", "dc")
    return jax.shard_map(
        layer,
        mesh=inner,
        in_specs=(
            P(dp, "mp"),
            P(),
            P(dp, "mp"),
            P(dp, "mp"),
            P(dp, "mp"),
            P("mp"),
            P("mp"),
            P("mp"),
            P(),
            P(),
            P(),
            P(),
            P(dp, None, "mp"),
            P(dp, None, "mp"),
            P(dp, None, None, None, "mp"),
            P(dp, None),
        ),
        out_specs=(P(dp, "mp"), P(dp, None, None, None, "mp")),
        check_vma=False,
    )
```

```python
import functools
import math

import jax
import jax.numpy as jnp
from jax import lax
from jax.experimental import pallas as pl
from jax.experimental.pallas import tpu as pltpu
from jax.sharding import Mesh, PartitionSpec as P

HD = 128
CAP = 2
Q_TILE = 1024
K_TILE = 512
MAX_REQUEST = 3072


NEG_BIG = -1e30
EPSILON = 1e-06
THETA = 1000000.0


def rotary(values, positions):
    head_dim = values.shape[-1]
    half_dim = head_dim // 2
    frequency = jnp.exp(
        -jnp.arange(half_dim, dtype=jnp.float32) * (2.0 / head_dim) * math.log(THETA)
    )
    angles = positions[:, None] * frequency[None, :]
    cosine = jnp.concatenate([jnp.cos(angles), jnp.cos(angles)], axis=-1)[:, None, :]
    sine_part = jnp.concatenate([jnp.sin(angles), jnp.sin(angles)], axis=-1)[:, None, :]
    first_half = values[..., :half_dim]
    second_half = values[..., half_dim:]
    turned = jnp.concatenate([-second_half, first_half], axis=-1)
    return values * cosine + turned * sine_part


def request_index(rows_here, ends_at):
    return jnp.sum((rows_here[:, None] >= ends_at[None, :]).astype(jnp.int32), axis=1)


def token_table(global_rows, request_lens, request_group, prompt_lens):
    ends_at = jnp.cumsum(request_lens)
    starts_at = ends_at - request_lens
    request_of = request_index(global_rows, ends_at)
    one_hot = request_of[:, None] == jnp.arange(request_lens.shape[0], dtype=jnp.int32)[None, :]
    first_row = jnp.sum(jnp.where(one_hot, starts_at[None, :], 0), axis=1)
    group_of = jnp.sum(jnp.where(one_hot, request_group[None, :], 0), axis=1)
    group_hot = group_of[:, None] == jnp.arange(prompt_lens.shape[0], dtype=jnp.int32)[None, :]
    prefix_of = jnp.sum(jnp.where(group_hot, prompt_lens[None, :], 0), axis=1)
    positions = (prefix_of + global_rows - first_row).astype(jnp.float32)
    return (request_of, group_hot, positions, ends_at)


def prompt_mask(prompt_table, prompt_lens, block_count, block_size):
    blocks = jnp.arange(block_count, dtype=jnp.int32)
    matching = prompt_table[:, :, None] == blocks[None, None, :]
    present = jnp.any(matching, axis=1)
    slot_no = jnp.sum(
        jnp.where(matching, jnp.arange(prompt_table.shape[1], dtype=jnp.int32)[None, :, None], 0),
        axis=1,
    )
    within = (
        slot_no[:, :, None] * block_size + jnp.arange(block_size, dtype=jnp.int32)[None, None, :]
    )
    allowed = present[:, :, None] & (within < prompt_lens[:, None, None])
    return allowed.reshape(prompt_table.shape[0], block_count * block_size)


def attend(current, queries, keys_flat, values_flat, allowed, score_scale):
    best_score, total_sum, accumulated = current
    scores = (
        jnp.einsum("kgqd,skd->kgqs", queries, keys_flat, preferred_element_type=jnp.float32)
        * score_scale
    )
    masked = allowed[None, None, :, :]
    scores = jnp.where(masked, scores, NEG_BIG)
    new_best = jnp.maximum(best_score, jnp.max(scores, axis=-1))
    weights = jnp.where(masked, jnp.exp(scores - new_best[..., None]), 0.0)
    factor = jnp.exp(best_score - new_best)
    total_sum = total_sum * factor + jnp.sum(weights, axis=-1)
    accumulated = accumulated * factor[..., None] + jnp.einsum(
        "kgqs,skd->kgqd",
        weights.astype(jnp.bfloat16),
        values_flat,
        preferred_element_type=jnp.float32,
    )
    return (new_best, total_sum, accumulated)


def flash_kernel(flags, grp_ref, lo_ref, hi_ref, tag_ref, key_row_ref, q_ref, k_ref, v_ref,
                 o_ref, acc, m_sc, l_sc, *, scale):
    qi = pl.program_id(0)
    kj = pl.program_id(1)

    @pl.when(kj == 0)
    def _():
        m_sc[...] = jnp.full(m_sc.shape, NEG_BIG, jnp.float32)
        l_sc[...] = jnp.zeros(l_sc.shape, jnp.float32)
        acc[...] = jnp.zeros(acc.shape, jnp.float32)

    @pl.when(flags[qi, kj] > 0)
    def _():
        s = lax.dot_general(q_ref[...], k_ref[...], (((1,), (1,)), ((), ())),
                            preferred_element_type=jnp.float32) * scale
        tag = tag_ref[0:1, :]
        key_row = key_row_ref[0:1, :]
        allowed = (tag == grp_ref[...]) | ((key_row >= lo_ref[...]) & (key_row <= hi_ref[...]))
        s = jnp.where(allowed, s, NEG_BIG)
        m_prev = m_sc[:, 0:1]
        m_new = jnp.maximum(m_prev, jnp.max(s, axis=1, keepdims=True))
        p = jnp.where(allowed, jnp.exp(s - m_new), 0.0)
        alpha = jnp.exp(m_prev - m_new)
        l_sc[...] = jnp.broadcast_to(alpha * l_sc[:, 0:1] + jnp.sum(p, axis=1, keepdims=True), l_sc.shape)
        m_sc[...] = jnp.broadcast_to(m_new, m_sc.shape)
        acc[...] = acc[...] * alpha + jnp.dot(p.astype(jnp.bfloat16), v_ref[...],
                                              preferred_element_type=jnp.float32)

    @pl.when(kj == pl.num_programs(1) - 1)
    def _():
        o_ref[...] = (acc[...] / l_sc[:, 0:1]).astype(o_ref.dtype)


def flash(q, k, v, grp, lo, hi, tag, key_row, flags, tq, tk, scale):
    rows, hd = q.shape
    keys = k.shape[0]
    nq, nk = rows // tq, keys // tk
    row_spec = pl.BlockSpec((tq, 1), lambda i, j, f: (i, 0))
    key_spec = pl.BlockSpec((1, tk), lambda i, j, f: (0, j))
    grid_spec = pltpu.PrefetchScalarGridSpec(
        num_scalar_prefetch=1,
        grid=(nq, nk),
        in_specs=[row_spec, row_spec, row_spec, key_spec, key_spec,
                  pl.BlockSpec((tq, hd), lambda i, j, f: (i, 0)),
                  pl.BlockSpec((tk, hd), lambda i, j, f: (j, 0)),
                  pl.BlockSpec((tk, hd), lambda i, j, f: (j, 0))],
        out_specs=pl.BlockSpec((tq, hd), lambda i, j, f: (i, 0)),
        scratch_shapes=[pltpu.VMEM((tq, hd), jnp.float32),
                        pltpu.VMEM((tq, 128), jnp.float32),
                        pltpu.VMEM((tq, 128), jnp.float32)],
    )
    return pl.pallas_call(
        functools.partial(flash_kernel, scale=scale),
        grid_spec=grid_spec,
        out_shape=jax.ShapeDtypeStruct((rows, hd), jnp.bfloat16),
    )(flags, grp, lo, hi, tag, key_row, q, k, v)


def dp_index():
    return lax.axis_index("dz") * lax.axis_size("dc") + lax.axis_index("dc")


def relayout(prev_cache, dest_device):
    blocks_here = prev_cache.shape[0]
    devices = lax.axis_size("dz") * lax.axis_size("dc")
    slot_count = devices * CAP
    target = dest_device[:, 0]
    same_target = target[:, None] == target[None, :]
    earlier = (
        jnp.arange(blocks_here, dtype=jnp.int32)[None, :]
        < jnp.arange(blocks_here, dtype=jnp.int32)[:, None]
    )
    block_rank = jnp.sum((same_target & earlier).astype(jnp.int32), axis=1)
    slot_device = jnp.arange(slot_count, dtype=jnp.int32) // CAP
    slot_rank = jnp.arange(slot_count, dtype=jnp.int32) % CAP
    matches = (target[None, :] == slot_device[:, None]) & (
        block_rank[None, :] == slot_rank[:, None]
    )
    filled = jnp.any(matches, axis=1)
    source = jnp.sum(
        jnp.where(matches, jnp.arange(blocks_here, dtype=jnp.int32)[None, :], 0), axis=1
    )
    packed = jnp.take(prev_cache, source, axis=0)
    slot_flags = filled.astype(jnp.bfloat16)
    arrived, arrived_flags = (
        lax.all_to_all(packed, ("dz", "dc"), split_axis=0, concat_axis=0, tiled=True),
        lax.all_to_all(slot_flags, ("dz", "dc"), split_axis=0, concat_axis=0, tiled=True),
    )
    arrived_live = arrived_flags > 0.5
    order_no = jnp.cumsum(arrived_live.astype(jnp.int32)) - 1
    picked = arrived_live[None, :] & (
        order_no[None, :] == jnp.arange(blocks_here, dtype=jnp.int32)[:, None]
    )
    chosen = jnp.sum(jnp.where(picked, jnp.arange(slot_count, dtype=jnp.int32)[None, :], 0), axis=1)
    return jnp.take(arrived, chosen, axis=0)


def per_device(
    hidden,
    norm_gain,
    query_weight,
    key_weight,
    value_weight,
    query_bias,
    key_bias,
    value_bias,
    request_lens,
    request_group,
    prompt_lens,
    prompt_table,
    pool_keys,
    pool_values,
    prev_cache,
    dest_device,
):
    row_count = hidden.shape[0]
    me = dp_index()
    side = lax.axis_index("dc")
    sides = lax.axis_size("dc")
    global_rows = me * row_count + jnp.arange(row_count, dtype=jnp.int32)
    request_of, group_hot, positions, ends_at = token_table(
        global_rows, request_lens, request_group, prompt_lens
    )
    mp_size = lax.axis_size("mp")
    spread = jnp.broadcast_to(hidden[None], (mp_size,) + hidden.shape)
    pieces = lax.all_to_all(spread, "mp", split_axis=0, concat_axis=0, tiled=True)
    q_cols = query_weight.shape[1]
    k_cols = key_weight.shape[1]
    block_rows = query_weight.shape[0]
    pool_here = jnp.concatenate([pool_keys, pool_values], axis=2).reshape(block_rows, -1)
    weights_here = jnp.concatenate([query_weight, key_weight, value_weight, pool_here], axis=1)
    weights_all = lax.all_gather(weights_here, ("dz", "dc"), axis=0, tiled=True)
    proj_cols = q_cols + 2 * k_cols
    pool_all = weights_all[:, proj_cols:].reshape(
        (-1,) + pool_keys.shape[1:2] + (2 * pool_keys.shape[2],)
    )
    as_float = pieces.astype(jnp.float32)
    inverse = lax.rsqrt(
        jnp.mean(jnp.sum(as_float * as_float, axis=2), axis=0)[None, :, None] / pieces.shape[2]
        + EPSILON
    )
    gain = norm_gain.astype(jnp.float32).reshape(mp_size, 1, -1)
    normed = (as_float * inverse * gain).astype(jnp.bfloat16)
    proj = jnp.einsum(
        "jtf,jfc->tc",
        normed,
        weights_all.reshape(mp_size, -1, weights_all.shape[1]),
        preferred_element_type=jnp.float32,
    )
    query_proj = proj[:, :q_cols] + query_bias.astype(jnp.float32)[None, :]
    key_proj = proj[:, q_cols:q_cols + k_cols] + key_bias.astype(jnp.float32)[None, :]
    value_proj = proj[:, q_cols + k_cols:proj_cols] + value_bias.astype(jnp.float32)[None, :]
    local_heads = query_proj.shape[1] // HD
    local_kv = key_proj.shape[1] // HD
    group_size = local_heads // local_kv
    queries = rotary(query_proj.reshape(row_count, local_heads, HD), positions).astype(jnp.bfloat16)
    queries = queries.reshape(row_count * local_heads, HD)
    keys_new = (
        rotary(key_proj.reshape(row_count, local_kv, HD), positions)
        .astype(jnp.bfloat16)
        .reshape(row_count, local_kv * HD)
    )
    values_new = value_proj.astype(jnp.bfloat16)
    span_here = jnp.concatenate([keys_new, values_new], axis=1)
    span_all = lax.all_gather(span_here, ("dz", "dc"), axis=0, tiled=True)
    prev_cache, span_all = lax.optimization_barrier((prev_cache, span_all))
    decode_cache = relayout(prev_cache, dest_device)
    score_scale = HD ** (-0.5)
    block_size = pool_all.shape[1]
    blocks_here = pool_all.shape[0]
    kv_width = local_kv * HD
    key_count = span_all.shape[0]
    window = min(key_count, MAX_REQUEST + row_count)
    window = -(-window // K_TILE) * K_TILE
    window_start = jnp.maximum((me + 1) * row_count - window, 0)
    span_window = lax.dynamic_slice_in_dim(span_all, window_start, window, axis=0)
    pool_flat = pool_all.reshape(blocks_here * block_size, 2 * kv_width)
    all_keys = jnp.concatenate([pool_flat[:, :kv_width], span_window[:, :kv_width]], axis=0)
    all_values = jnp.concatenate([pool_flat[:, kv_width:], span_window[:, kv_width:]], axis=0)
    blocks = jnp.arange(blocks_here, dtype=jnp.int32)
    matching = prompt_table[:, :, None] == blocks[None, None, :]
    slot_no = jnp.sum(
        jnp.where(matching, jnp.arange(prompt_table.shape[1], dtype=jnp.int32)[None, :, None], 0),
        axis=(0, 1),
    )
    group_no = jnp.sum(
        jnp.where(matching, jnp.arange(prompt_table.shape[0], dtype=jnp.int32)[:, None, None], 0),
        axis=(0, 1),
    )
    named = jnp.any(matching, axis=(0, 1))
    within = slot_no[:, None] * block_size + jnp.arange(block_size, dtype=jnp.int32)[None, :]
    block_len = jnp.take(prompt_lens, group_no)
    pool_tag = jnp.where(named[:, None] & (within < block_len[:, None]), group_no[:, None], -1)
    key_tag = jnp.concatenate(
        [pool_tag.reshape(-1), jnp.full((window,), -2, jnp.int32)]
    )
    key_row = jnp.concatenate(
        [
            jnp.full((blocks_here * block_size,), -1, jnp.int32),
            window_start + jnp.arange(window, dtype=jnp.int32),
        ]
    )
    starts_at = ends_at - request_lens
    token_group = jnp.take(request_group, request_of)
    token_start = jnp.take(starts_at, request_of)
    seen = (key_tag[None, :] == token_group[:, None]) | (
        (key_row[None, :] >= token_start[:, None]) & (key_row[None, :] <= global_rows[:, None])
    )
    q_tokens = Q_TILE // local_heads
    flags = jnp.any(
        seen.reshape(row_count // q_tokens, q_tokens, -1, K_TILE), axis=(1, 3)
    ).astype(jnp.int32)

    def per_row(x):
        return jnp.repeat(x, local_heads)[:, None]

    output = flash(
        queries,
        all_keys,
        all_values,
        per_row(token_group),
        per_row(token_start),
        per_row(global_rows),
        key_tag[None, :],
        key_row[None, :],
        flags,
        Q_TILE,
        K_TILE,
        score_scale,
    )
    context = output.reshape(row_count, local_heads * HD)
    return (context, decode_cache)


def solution(mesh):
    dp_size, mp_size = mesh.devices.shape
    inner = Mesh(mesh.devices.reshape(dp_size // 2, 2, mp_size), ("dz", "dc", "mp"))
    dp = ("dz", "dc")
    return jax.shard_map(
        per_device,
        mesh=inner,
        in_specs=(
            P(dp, "mp"),
            P(),
            P(dp, "mp"),
            P(dp, "mp"),
            P(dp, "mp"),
            P("mp"),
            P("mp"),
            P("mp"),
            P(),
            P(),
            P(),
            P(),
            P(dp, None, "mp"),
            P(dp, None, "mp"),
            P(dp, None, None, None, "mp"),
            P(dp, None),
        ),
        out_specs=(P(dp, "mp"), P(dp, None, None, None, "mp")),
        check_vma=False,
    )
```

```python
import functools
import math

import jax
import jax.numpy as jnp
from jax import lax
from jax.experimental import pallas as pl
from jax.experimental.pallas import tpu as pltpu
from jax.sharding import Mesh, PartitionSpec as P

HD = 128
CAP = 2
Q_TILE = 1024
K_TILE = 512
MAX_REQUEST = 3072


NEG_BIG = -1e30
EPSILON = 1e-06
THETA = 1000000.0


def rotary(values, positions):
    head_dim = values.shape[-1]
    half_dim = head_dim // 2
    frequency = jnp.exp(
        -jnp.arange(half_dim, dtype=jnp.float32) * (2.0 / head_dim) * math.log(THETA)
    )
    angles = positions[:, None] * frequency[None, :]
    cosine = jnp.concatenate([jnp.cos(angles), jnp.cos(angles)], axis=-1)[:, None, :]
    sine_part = jnp.concatenate([jnp.sin(angles), jnp.sin(angles)], axis=-1)[:, None, :]
    first_half = values[..., :half_dim]
    second_half = values[..., half_dim:]
    turned = jnp.concatenate([-second_half, first_half], axis=-1)
    return values * cosine + turned * sine_part


def request_index(rows_here, ends_at):
    return jnp.sum((rows_here[:, None] >= ends_at[None, :]).astype(jnp.int32), axis=1)


def token_table(global_rows, request_lens, request_group, prompt_lens):
    ends_at = jnp.cumsum(request_lens)
    starts_at = ends_at - request_lens
    request_of = request_index(global_rows, ends_at)
    one_hot = request_of[:, None] == jnp.arange(request_lens.shape[0], dtype=jnp.int32)[None, :]
    first_row = jnp.sum(jnp.where(one_hot, starts_at[None, :], 0), axis=1)
    group_of = jnp.sum(jnp.where(one_hot, request_group[None, :], 0), axis=1)
    group_hot = group_of[:, None] == jnp.arange(prompt_lens.shape[0], dtype=jnp.int32)[None, :]
    prefix_of = jnp.sum(jnp.where(group_hot, prompt_lens[None, :], 0), axis=1)
    positions = (prefix_of + global_rows - first_row).astype(jnp.float32)
    return (request_of, group_hot, positions, ends_at)


def prompt_mask(prompt_table, prompt_lens, block_count, block_size):
    blocks = jnp.arange(block_count, dtype=jnp.int32)
    matching = prompt_table[:, :, None] == blocks[None, None, :]
    present = jnp.any(matching, axis=1)
    slot_no = jnp.sum(
        jnp.where(matching, jnp.arange(prompt_table.shape[1], dtype=jnp.int32)[None, :, None], 0),
        axis=1,
    )
    within = (
        slot_no[:, :, None] * block_size + jnp.arange(block_size, dtype=jnp.int32)[None, None, :]
    )
    allowed = present[:, :, None] & (within < prompt_lens[:, None, None])
    return allowed.reshape(prompt_table.shape[0], block_count * block_size)


def attend(current, queries, keys_flat, values_flat, allowed, score_scale):
    best_score, total_sum, accumulated = current
    scores = (
        jnp.einsum("kgqd,skd->kgqs", queries, keys_flat, preferred_element_type=jnp.float32)
        * score_scale
    )
    masked = allowed[None, None, :, :]
    scores = jnp.where(masked, scores, NEG_BIG)
    new_best = jnp.maximum(best_score, jnp.max(scores, axis=-1))
    weights = jnp.where(masked, jnp.exp(scores - new_best[..., None]), 0.0)
    factor = jnp.exp(best_score - new_best)
    total_sum = total_sum * factor + jnp.sum(weights, axis=-1)
    accumulated = accumulated * factor[..., None] + jnp.einsum(
        "kgqs,skd->kgqd",
        weights.astype(jnp.bfloat16),
        values_flat,
        preferred_element_type=jnp.float32,
    )
    return (new_best, total_sum, accumulated)


def flash_kernel(flags, grp_ref, lo_ref, hi_ref, tag_ref, key_row_ref, q_ref, k_ref, v_ref,
                 o_ref, acc, m_sc, l_sc, *, scale):
    qi = pl.program_id(0)
    kj = pl.program_id(1)

    @pl.when(kj == 0)
    def _():
        m_sc[...] = jnp.full(m_sc.shape, NEG_BIG, jnp.float32)
        l_sc[...] = jnp.zeros(l_sc.shape, jnp.float32)
        acc[...] = jnp.zeros(acc.shape, jnp.float32)

    @pl.when(flags[qi, kj] > 0)
    def _():
        s = lax.dot_general(q_ref[...], k_ref[...], (((1,), (1,)), ((), ())),
                            preferred_element_type=jnp.float32) * scale
        tag = tag_ref[0:1, :]
        key_row = key_row_ref[0:1, :]
        allowed = (tag == grp_ref[...]) | ((key_row >= lo_ref[...]) & (key_row <= hi_ref[...]))
        s = jnp.where(allowed, s, NEG_BIG)
        m_prev = m_sc[:, 0:1]
        m_new = jnp.maximum(m_prev, jnp.max(s, axis=1, keepdims=True))
        p = jnp.where(allowed, jnp.exp(s - m_new), 0.0)
        alpha = jnp.exp(m_prev - m_new)
        l_sc[...] = jnp.broadcast_to(alpha * l_sc[:, 0:1] + jnp.sum(p, axis=1, keepdims=True), l_sc.shape)
        m_sc[...] = jnp.broadcast_to(m_new, m_sc.shape)
        acc[...] = acc[...] * alpha + jnp.dot(p.astype(jnp.bfloat16), v_ref[...],
                                              preferred_element_type=jnp.float32)

    @pl.when(kj == pl.num_programs(1) - 1)
    def _():
        o_ref[...] = (acc[...] / l_sc[:, 0:1]).astype(o_ref.dtype)


def flash(q, k, v, grp, lo, hi, tag, key_row, flags, tq, tk, scale):
    rows, hd = q.shape
    keys = k.shape[0]
    nq, nk = rows // tq, keys // tk
    row_spec = pl.BlockSpec((tq, 1), lambda i, j, f: (i, 0))
    key_spec = pl.BlockSpec((1, tk), lambda i, j, f: (0, j))
    grid_spec = pltpu.PrefetchScalarGridSpec(
        num_scalar_prefetch=1,
        grid=(nq, nk),
        in_specs=[row_spec, row_spec, row_spec, key_spec, key_spec,
                  pl.BlockSpec((tq, hd), lambda i, j, f: (i, 0)),
                  pl.BlockSpec((tk, hd), lambda i, j, f: (j, 0)),
                  pl.BlockSpec((tk, hd), lambda i, j, f: (j, 0))],
        out_specs=pl.BlockSpec((tq, hd), lambda i, j, f: (i, 0)),
        scratch_shapes=[pltpu.VMEM((tq, hd), jnp.float32),
                        pltpu.VMEM((tq, 128), jnp.float32),
                        pltpu.VMEM((tq, 128), jnp.float32)],
    )
    return pl.pallas_call(
        functools.partial(flash_kernel, scale=scale),
        grid_spec=grid_spec,
        out_shape=jax.ShapeDtypeStruct((rows, hd), jnp.bfloat16),
    )(flags, grp, lo, hi, tag, key_row, q, k, v)


def dp_index():
    return lax.axis_index("dz") * lax.axis_size("dc") + lax.axis_index("dc")


def pack_cache(prev_cache, dest_device):
    blocks_here = prev_cache.shape[0]
    devices = lax.axis_size("dz") * lax.axis_size("dc")
    slot_count = devices * CAP
    target = dest_device[:, 0]
    same_target = target[:, None] == target[None, :]
    earlier = (
        jnp.arange(blocks_here, dtype=jnp.int32)[None, :]
        < jnp.arange(blocks_here, dtype=jnp.int32)[:, None]
    )
    block_rank = jnp.sum((same_target & earlier).astype(jnp.int32), axis=1)
    slot_device = jnp.arange(slot_count, dtype=jnp.int32) // CAP
    slot_rank = jnp.arange(slot_count, dtype=jnp.int32) % CAP
    matches = (target[None, :] == slot_device[:, None]) & (
        block_rank[None, :] == slot_rank[:, None]
    )
    filled = jnp.any(matches, axis=1)
    source = jnp.sum(
        jnp.where(matches, jnp.arange(blocks_here, dtype=jnp.int32)[None, :], 0), axis=1
    )
    packed = jnp.take(prev_cache, source, axis=0, mode="clip")
    slot_flags = filled.astype(jnp.bfloat16)
    return packed, slot_flags


def unpack_cache(packed, slot_flags):
    blocks_here = packed.shape[0] // CAP
    slot_count = packed.shape[0]
    arrived, arrived_flags = (
        lax.all_to_all(packed, ("dz", "dc"), split_axis=0, concat_axis=0, tiled=True),
        lax.all_to_all(slot_flags, ("dz", "dc"), split_axis=0, concat_axis=0, tiled=True),
    )
    arrived_live = arrived_flags > 0.5
    order_no = jnp.cumsum(arrived_live.astype(jnp.int32)) - 1
    picked = arrived_live[None, :] & (
        order_no[None, :] == jnp.arange(blocks_here, dtype=jnp.int32)[:, None]
    )
    chosen = jnp.sum(jnp.where(picked, jnp.arange(slot_count, dtype=jnp.int32)[None, :], 0), axis=1)
    return jnp.take(arrived, chosen, axis=0, mode="clip")


def per_device(
    hidden,
    norm_gain,
    query_weight,
    key_weight,
    value_weight,
    query_bias,
    key_bias,
    value_bias,
    request_lens,
    request_group,
    prompt_lens,
    prompt_table,
    pool_keys,
    pool_values,
    prev_cache,
    dest_device,
):
    row_count = hidden.shape[0]
    me = dp_index()
    side = lax.axis_index("dc")
    sides = lax.axis_size("dc")
    global_rows = me * row_count + jnp.arange(row_count, dtype=jnp.int32)
    request_of, group_hot, positions, ends_at = token_table(
        global_rows, request_lens, request_group, prompt_lens
    )
    mp_size = lax.axis_size("mp")
    spread = jnp.broadcast_to(hidden[None], (mp_size,) + hidden.shape)
    pieces = lax.all_to_all(spread, "mp", split_axis=0, concat_axis=0, tiled=True)
    local_heads = query_weight.shape[1] // HD
    local_kv = key_weight.shape[1] // HD
    block_size = pool_keys.shape[1]
    blocks_here = pool_keys.shape[0] * lax.axis_size("dz") * lax.axis_size("dc")
    key_count = row_count * lax.axis_size("dz") * lax.axis_size("dc")
    window = min(key_count, MAX_REQUEST + row_count)
    window = -(-window // K_TILE) * K_TILE
    window_start = jnp.maximum((me + 1) * row_count - window, 0)
    blocks = jnp.arange(blocks_here, dtype=jnp.int32)
    matching = prompt_table[:, :, None] == blocks[None, None, :]
    slot_no = jnp.sum(
        jnp.where(matching, jnp.arange(prompt_table.shape[1], dtype=jnp.int32)[None, :, None], 0),
        axis=(0, 1),
    )
    group_no = jnp.sum(
        jnp.where(matching, jnp.arange(prompt_table.shape[0], dtype=jnp.int32)[:, None, None], 0),
        axis=(0, 1),
    )
    named = jnp.any(matching, axis=(0, 1))
    within = slot_no[:, None] * block_size + jnp.arange(block_size, dtype=jnp.int32)[None, :]
    block_len = jnp.take(prompt_lens, group_no)
    pool_tag = jnp.where(named[:, None] & (within < block_len[:, None]), group_no[:, None], -1)
    key_tag = jnp.concatenate(
        [pool_tag.reshape(-1), jnp.full((window,), -2, jnp.int32)]
    )
    key_row = jnp.concatenate(
        [
            jnp.full((blocks_here * block_size,), -1, jnp.int32),
            window_start + jnp.arange(window, dtype=jnp.int32),
        ]
    )
    starts_at = ends_at - request_lens
    token_group = jnp.take(request_group, request_of)
    token_start = jnp.take(starts_at, request_of)
    seen = (key_tag[None, :] == token_group[:, None]) | (
        (key_row[None, :] >= token_start[:, None]) & (key_row[None, :] <= global_rows[:, None])
    )
    q_tokens = Q_TILE // local_heads
    flags = jnp.any(
        seen.reshape(row_count // q_tokens, q_tokens, -1, K_TILE), axis=(1, 3)
    ).astype(jnp.int32)


    def per_row(x):
        return jnp.repeat(x, local_heads)[:, None]

    row_group, row_start, row_last = per_row(token_group), per_row(token_start), per_row(global_rows)
    key_tag, key_row = key_tag[None, :], key_row[None, :]
    packed, slot_flags = pack_cache(prev_cache, dest_device)
    pieces, packed, slot_flags, row_group, row_start, row_last, key_tag, key_row, flags, positions = (
        lax.optimization_barrier(
            (pieces, packed, slot_flags, row_group, row_start, row_last, key_tag, key_row, flags,
             positions)
        )
    )
    q_cols = query_weight.shape[1]
    k_cols = key_weight.shape[1]
    block_rows = query_weight.shape[0]
    pool_here = jnp.concatenate([pool_keys, pool_values], axis=2).reshape(block_rows, -1)
    weights_here = jnp.concatenate([query_weight, key_weight, value_weight, pool_here], axis=1)
    weights_all = lax.all_gather(weights_here, ("dz", "dc"), axis=0, tiled=True)
    packed, weights_all = lax.optimization_barrier((packed, weights_all))
    decode_cache = unpack_cache(packed, slot_flags)
    proj_cols = q_cols + 2 * k_cols
    pool_all = weights_all[:, proj_cols:].reshape(
        (-1,) + pool_keys.shape[1:2] + (2 * pool_keys.shape[2],)
    )
    as_float = pieces.astype(jnp.float32)
    inverse = lax.rsqrt(
        jnp.mean(jnp.sum(as_float * as_float, axis=2), axis=0)[None, :, None] / pieces.shape[2]
        + EPSILON
    )
    gain = norm_gain.astype(jnp.float32).reshape(mp_size, 1, -1)
    normed = (as_float * inverse * gain).astype(jnp.bfloat16)
    proj = jnp.einsum(
        "jtf,jfc->tc",
        normed,
        weights_all.reshape(mp_size, -1, weights_all.shape[1]),
        preferred_element_type=jnp.float32,
    )
    query_proj = proj[:, :q_cols] + query_bias.astype(jnp.float32)[None, :]
    key_proj = proj[:, q_cols:q_cols + k_cols] + key_bias.astype(jnp.float32)[None, :]
    value_proj = proj[:, q_cols + k_cols:proj_cols] + value_bias.astype(jnp.float32)[None, :]
    queries = rotary(query_proj.reshape(row_count, local_heads, HD), positions).astype(jnp.bfloat16)
    queries = queries.reshape(row_count * local_heads, HD)
    keys_new = (
        rotary(key_proj.reshape(row_count, local_kv, HD), positions)
        .astype(jnp.bfloat16)
        .reshape(row_count, local_kv * HD)
    )
    values_new = value_proj.astype(jnp.bfloat16)
    span_here = jnp.concatenate([keys_new, values_new], axis=1)
    span_all = lax.all_gather(span_here, ("dz", "dc"), axis=0, tiled=True)
    score_scale = HD ** (-0.5)
    kv_width = local_kv * HD
    span_window = lax.dynamic_slice_in_dim(span_all, window_start, window, axis=0)
    pool_flat = pool_all.reshape(blocks_here * block_size, 2 * kv_width)
    all_keys = jnp.concatenate([pool_flat[:, :kv_width], span_window[:, :kv_width]], axis=0)
    all_values = jnp.concatenate([pool_flat[:, kv_width:], span_window[:, kv_width:]], axis=0)
    output = flash(
        queries,
        all_keys,
        all_values,
        row_group,
        row_start,
        row_last,
        key_tag,
        key_row,
        flags,
        Q_TILE,
        K_TILE,
        score_scale,
    )
    context = output.reshape(row_count, local_heads * HD)
    return (context, decode_cache)


def solution(mesh):
    dp_size, mp_size = mesh.devices.shape
    inner = Mesh(mesh.devices.reshape(dp_size // 2, 2, mp_size), ("dz", "dc", "mp"))
    dp = ("dz", "dc")
    return jax.shard_map(
        per_device,
        mesh=inner,
        in_specs=(
            P(dp, "mp"),
            P(),
            P(dp, "mp"),
            P(dp, "mp"),
            P(dp, "mp"),
            P("mp"),
            P("mp"),
            P("mp"),
            P(),
            P(),
            P(),
            P(),
            P(dp, None, "mp"),
            P(dp, None, "mp"),
            P(dp, None, None, None, "mp"),
            P(dp, None),
        ),
        out_specs=(P(dp, "mp"), P(dp, None, None, None, "mp")),
        check_vma=False,
    )
```

```python
import functools
import math

import jax
import jax.numpy as jnp
from jax import lax
from jax.experimental import pallas as pl
from jax.experimental.pallas import tpu as pltpu
from jax.sharding import Mesh, PartitionSpec as P

HD = 128
CAP = 2
Q_TILE = 1024
K_TILE = 512
MAX_REQUEST = 3072


NEG_BIG = -1e30
EPSILON = 1e-06
THETA = 1000000.0


def rotary(values, positions):
    head_dim = values.shape[-1]
    half_dim = head_dim // 2
    frequency = jnp.exp(
        -jnp.arange(half_dim, dtype=jnp.float32) * (2.0 / head_dim) * math.log(THETA)
    )
    angles = positions[:, None] * frequency[None, :]
    cosine = jnp.concatenate([jnp.cos(angles), jnp.cos(angles)], axis=-1)[:, None, :]
    sine_part = jnp.concatenate([jnp.sin(angles), jnp.sin(angles)], axis=-1)[:, None, :]
    first_half = values[..., :half_dim]
    second_half = values[..., half_dim:]
    turned = jnp.concatenate([-second_half, first_half], axis=-1)
    return values * cosine + turned * sine_part


def request_index(rows_here, ends_at):
    return jnp.sum((rows_here[:, None] >= ends_at[None, :]).astype(jnp.int32), axis=1)


def token_table(global_rows, request_lens, request_group, prompt_lens):
    ends_at = jnp.cumsum(request_lens)
    starts_at = ends_at - request_lens
    request_of = request_index(global_rows, ends_at)
    one_hot = request_of[:, None] == jnp.arange(request_lens.shape[0], dtype=jnp.int32)[None, :]
    first_row = jnp.sum(jnp.where(one_hot, starts_at[None, :], 0), axis=1)
    group_of = jnp.sum(jnp.where(one_hot, request_group[None, :], 0), axis=1)
    group_hot = group_of[:, None] == jnp.arange(prompt_lens.shape[0], dtype=jnp.int32)[None, :]
    prefix_of = jnp.sum(jnp.where(group_hot, prompt_lens[None, :], 0), axis=1)
    positions = (prefix_of + global_rows - first_row).astype(jnp.float32)
    return (request_of, group_hot, positions, ends_at)


def prompt_mask(prompt_table, prompt_lens, block_count, block_size):
    blocks = jnp.arange(block_count, dtype=jnp.int32)
    matching = prompt_table[:, :, None] == blocks[None, None, :]
    present = jnp.any(matching, axis=1)
    slot_no = jnp.sum(
        jnp.where(matching, jnp.arange(prompt_table.shape[1], dtype=jnp.int32)[None, :, None], 0),
        axis=1,
    )
    within = (
        slot_no[:, :, None] * block_size + jnp.arange(block_size, dtype=jnp.int32)[None, None, :]
    )
    allowed = present[:, :, None] & (within < prompt_lens[:, None, None])
    return allowed.reshape(prompt_table.shape[0], block_count * block_size)


def attend(current, queries, keys_flat, values_flat, allowed, score_scale):
    best_score, total_sum, accumulated = current
    scores = (
        jnp.einsum("kgqd,skd->kgqs", queries, keys_flat, preferred_element_type=jnp.float32)
        * score_scale
    )
    masked = allowed[None, None, :, :]
    scores = jnp.where(masked, scores, NEG_BIG)
    new_best = jnp.maximum(best_score, jnp.max(scores, axis=-1))
    weights = jnp.where(masked, jnp.exp(scores - new_best[..., None]), 0.0)
    factor = jnp.exp(best_score - new_best)
    total_sum = total_sum * factor + jnp.sum(weights, axis=-1)
    accumulated = accumulated * factor[..., None] + jnp.einsum(
        "kgqs,skd->kgqd",
        weights.astype(jnp.bfloat16),
        values_flat,
        preferred_element_type=jnp.float32,
    )
    return (new_best, total_sum, accumulated)


def flash_kernel(flags, grp_ref, lo_ref, hi_ref, tag_ref, key_row_ref, q_ref, k_ref, v_ref,
                 o_ref, acc, m_sc, l_sc, *, scale):
    qi = pl.program_id(0)
    kj = pl.program_id(1)

    @pl.when(kj == 0)
    def _():
        m_sc[...] = jnp.full(m_sc.shape, NEG_BIG, jnp.float32)
        l_sc[...] = jnp.zeros(l_sc.shape, jnp.float32)
        acc[...] = jnp.zeros(acc.shape, jnp.float32)

    @pl.when(flags[qi, kj] > 0)
    def _():
        s = lax.dot_general(q_ref[...], k_ref[...], (((1,), (1,)), ((), ())),
                            preferred_element_type=jnp.float32) * scale
        tag = tag_ref[0:1, :]
        key_row = key_row_ref[0:1, :]
        allowed = (tag == grp_ref[...]) | ((key_row >= lo_ref[...]) & (key_row <= hi_ref[...]))
        s = jnp.where(allowed, s, NEG_BIG)
        m_prev = m_sc[:, 0:1]
        m_new = jnp.maximum(m_prev, jnp.max(s, axis=1, keepdims=True))
        p = jnp.where(allowed, jnp.exp(s - m_new), 0.0)
        alpha = jnp.exp(m_prev - m_new)
        l_sc[...] = jnp.broadcast_to(alpha * l_sc[:, 0:1] + jnp.sum(p, axis=1, keepdims=True), l_sc.shape)
        m_sc[...] = jnp.broadcast_to(m_new, m_sc.shape)
        acc[...] = acc[...] * alpha + jnp.dot(p.astype(jnp.bfloat16), v_ref[...],
                                              preferred_element_type=jnp.float32)

    @pl.when(kj == pl.num_programs(1) - 1)
    def _():
        o_ref[...] = (acc[...] / l_sc[:, 0:1]).astype(o_ref.dtype)


def flash(q, k, v, grp, lo, hi, tag, key_row, flags, tq, tk, scale):
    rows, hd = q.shape
    keys = k.shape[0]
    nq, nk = rows // tq, keys // tk
    row_spec = pl.BlockSpec((tq, 1), lambda i, j, f: (i, 0))
    key_spec = pl.BlockSpec((1, tk), lambda i, j, f: (0, j))
    grid_spec = pltpu.PrefetchScalarGridSpec(
        num_scalar_prefetch=1,
        grid=(nq, nk),
        in_specs=[row_spec, row_spec, row_spec, key_spec, key_spec,
                  pl.BlockSpec((tq, hd), lambda i, j, f: (i, 0)),
                  pl.BlockSpec((tk, hd), lambda i, j, f: (j, 0)),
                  pl.BlockSpec((tk, hd), lambda i, j, f: (j, 0))],
        out_specs=pl.BlockSpec((tq, hd), lambda i, j, f: (i, 0)),
        scratch_shapes=[pltpu.VMEM((tq, hd), jnp.float32),
                        pltpu.VMEM((tq, 128), jnp.float32),
                        pltpu.VMEM((tq, 128), jnp.float32)],
    )
    return pl.pallas_call(
        functools.partial(flash_kernel, scale=scale),
        grid_spec=grid_spec,
        out_shape=jax.ShapeDtypeStruct((rows, hd), jnp.bfloat16),
    )(flags, grp, lo, hi, tag, key_row, q, k, v)


def dp_index():
    return lax.axis_index("dz") * lax.axis_size("dc") + lax.axis_index("dc")


def pack_cache(prev_cache, dest_device):
    blocks_here = prev_cache.shape[0]
    devices = lax.axis_size("dz") * lax.axis_size("dc")
    slot_count = devices * CAP
    target = dest_device[:, 0]
    same_target = target[:, None] == target[None, :]
    earlier = (
        jnp.arange(blocks_here, dtype=jnp.int32)[None, :]
        < jnp.arange(blocks_here, dtype=jnp.int32)[:, None]
    )
    block_rank = jnp.sum((same_target & earlier).astype(jnp.int32), axis=1)
    slot_device = jnp.arange(slot_count, dtype=jnp.int32) // CAP
    slot_rank = jnp.arange(slot_count, dtype=jnp.int32) % CAP
    matches = (target[None, :] == slot_device[:, None]) & (
        block_rank[None, :] == slot_rank[:, None]
    )
    filled = jnp.any(matches, axis=1)
    source = jnp.sum(
        jnp.where(matches, jnp.arange(blocks_here, dtype=jnp.int32)[None, :], 0), axis=1
    )
    packed = jnp.take(prev_cache, source, axis=0, mode="clip")
    slot_flags = filled.astype(jnp.bfloat16)
    return packed, slot_flags


def unpack_cache(packed, slot_flags):
    blocks_here = packed.shape[0] // CAP
    slot_count = packed.shape[0]
    arrived, arrived_flags = (
        lax.all_to_all(packed, ("dz", "dc"), split_axis=0, concat_axis=0, tiled=True),
        lax.all_to_all(slot_flags, ("dz", "dc"), split_axis=0, concat_axis=0, tiled=True),
    )
    arrived_live = arrived_flags > 0.5
    order_no = jnp.cumsum(arrived_live.astype(jnp.int32)) - 1
    picked = arrived_live[None, :] & (
        order_no[None, :] == jnp.arange(blocks_here, dtype=jnp.int32)[:, None]
    )
    chosen = jnp.sum(jnp.where(picked, jnp.arange(slot_count, dtype=jnp.int32)[None, :], 0), axis=1)
    return jnp.take(arrived, chosen, axis=0, mode="clip")


def per_device(
    hidden,
    norm_gain,
    query_weight,
    key_weight,
    value_weight,
    query_bias,
    key_bias,
    value_bias,
    request_lens,
    request_group,
    prompt_lens,
    prompt_table,
    pool_keys,
    pool_values,
    prev_cache,
    dest_device,
):
    row_count = hidden.shape[0]
    me = dp_index()
    side = lax.axis_index("dc")
    sides = lax.axis_size("dc")
    global_rows = me * row_count + jnp.arange(row_count, dtype=jnp.int32)
    request_of, group_hot, positions, ends_at = token_table(
        global_rows, request_lens, request_group, prompt_lens
    )
    mp_size = lax.axis_size("mp")
    full_rows = lax.all_gather(hidden, "mp", axis=1, tiled=True)
    local_heads = query_weight.shape[1] // HD
    local_kv = key_weight.shape[1] // HD
    block_size = pool_keys.shape[1]
    blocks_here = pool_keys.shape[0] * lax.axis_size("dz") * lax.axis_size("dc")
    key_count = row_count * lax.axis_size("dz") * lax.axis_size("dc")
    window = min(key_count, MAX_REQUEST + row_count)
    window = -(-window // K_TILE) * K_TILE
    window_start = jnp.maximum((me + 1) * row_count - window, 0)
    blocks = jnp.arange(blocks_here, dtype=jnp.int32)
    matching = prompt_table[:, :, None] == blocks[None, None, :]
    slot_no = jnp.sum(
        jnp.where(matching, jnp.arange(prompt_table.shape[1], dtype=jnp.int32)[None, :, None], 0),
        axis=(0, 1),
    )
    group_no = jnp.sum(
        jnp.where(matching, jnp.arange(prompt_table.shape[0], dtype=jnp.int32)[:, None, None], 0),
        axis=(0, 1),
    )
    named = jnp.any(matching, axis=(0, 1))
    within = slot_no[:, None] * block_size + jnp.arange(block_size, dtype=jnp.int32)[None, :]
    block_len = jnp.take(prompt_lens, group_no)
    pool_tag = jnp.where(named[:, None] & (within < block_len[:, None]), group_no[:, None], -1)
    key_tag = jnp.concatenate(
        [pool_tag.reshape(-1), jnp.full((window,), -2, jnp.int32)]
    )
    key_row = jnp.concatenate(
        [
            jnp.full((blocks_here * block_size,), -1, jnp.int32),
            window_start + jnp.arange(window, dtype=jnp.int32),
        ]
    )
    starts_at = ends_at - request_lens
    token_group = jnp.take(request_group, request_of)
    token_start = jnp.take(starts_at, request_of)
    seen = (key_tag[None, :] == token_group[:, None]) | (
        (key_row[None, :] >= token_start[:, None]) & (key_row[None, :] <= global_rows[:, None])
    )
    q_tokens = Q_TILE // local_heads
    flags = jnp.any(
        seen.reshape(row_count // q_tokens, q_tokens, -1, K_TILE), axis=(1, 3)
    ).astype(jnp.int32)


    def per_row(x):
        return jnp.repeat(x, local_heads)[:, None]

    row_group, row_start, row_last = per_row(token_group), per_row(token_start), per_row(global_rows)
    key_tag, key_row = key_tag[None, :], key_row[None, :]
    packed, slot_flags = pack_cache(prev_cache, dest_device)
    full_rows, packed, slot_flags, row_group, row_start, row_last, key_tag, key_row, flags, positions = (
        lax.optimization_barrier(
            (full_rows, packed, slot_flags, row_group, row_start, row_last, key_tag, key_row, flags,
             positions)
        )
    )
    q_cols = query_weight.shape[1]
    k_cols = key_weight.shape[1]
    block_rows = query_weight.shape[0]
    pool_here = jnp.concatenate([pool_keys, pool_values], axis=2).reshape(block_rows, -1)
    weights_here = jnp.concatenate([query_weight, key_weight, value_weight, pool_here], axis=1)
    nd = lax.axis_size("dz") * lax.axis_size("dc")
    half_rows = block_rows // 2
    halves = weights_here.reshape(2, half_rows, weights_here.shape[1])
    outgoing = jnp.tile(halves, (nd // 2, 1, 1))
    arrived_mine = lax.all_to_all(outgoing, ("dz", "dc"), split_axis=0, concat_axis=0, tiled=True)
    arrived_other = lax.ppermute(arrived_mine, "dc", perm=[(0, 1), (1, 0)])
    proj_cols = q_cols + 2 * k_cols
    first_is_mine = side == 0
    pool_first = jnp.where(first_is_mine, arrived_mine[:, :, proj_cols:], arrived_other[:, :, proj_cols:])
    pool_second = jnp.where(first_is_mine, arrived_other[:, :, proj_cols:], arrived_mine[:, :, proj_cols:])
    pool_all = jnp.concatenate([pool_first, pool_second], axis=1).reshape(
        (-1,) + pool_keys.shape[1:2] + (2 * pool_keys.shape[2],)
    )
    as_float = full_rows.astype(jnp.float32)
    inverse = lax.rsqrt(jnp.mean(as_float * as_float, axis=1, keepdims=True) + EPSILON)
    normed = (as_float * inverse * norm_gain.astype(jnp.float32)[None, :]).astype(jnp.bfloat16)
    normed_halves = normed.reshape(row_count, nd, 2, half_rows)
    normed_mine = lax.dynamic_index_in_dim(normed_halves, side, axis=2, keepdims=False)
    normed_other = lax.dynamic_index_in_dim(normed_halves, 1 - side, axis=2, keepdims=False)
    proj = jnp.dot(
        normed_mine.reshape(row_count, -1),
        arrived_mine.reshape(-1, arrived_mine.shape[2]),
        preferred_element_type=jnp.float32,
    ) + jnp.dot(
        normed_other.reshape(row_count, -1),
        arrived_other.reshape(-1, arrived_other.shape[2]),
        preferred_element_type=jnp.float32,
    )
    query_proj = proj[:, :q_cols] + query_bias.astype(jnp.float32)[None, :]
    key_proj = proj[:, q_cols:q_cols + k_cols] + key_bias.astype(jnp.float32)[None, :]
    value_proj = proj[:, q_cols + k_cols:proj_cols] + value_bias.astype(jnp.float32)[None, :]
    queries = rotary(query_proj.reshape(row_count, local_heads, HD), positions).astype(jnp.bfloat16)
    queries = queries.reshape(row_count * local_heads, HD)
    keys_new = (
        rotary(key_proj.reshape(row_count, local_kv, HD), positions)
        .astype(jnp.bfloat16)
        .reshape(row_count, local_kv * HD)
    )
    values_new = value_proj.astype(jnp.bfloat16)
    span_here = jnp.concatenate([keys_new, values_new], axis=1)
    span_all = lax.all_gather(span_here, ("dz", "dc"), axis=0, tiled=True)
    packed, span_all = lax.optimization_barrier((packed, span_all))
    decode_cache = unpack_cache(packed, slot_flags)
    score_scale = HD ** (-0.5)
    kv_width = local_kv * HD
    span_window = lax.dynamic_slice_in_dim(span_all, window_start, window, axis=0)
    pool_flat = pool_all.reshape(blocks_here * block_size, 2 * kv_width)
    all_keys = jnp.concatenate([pool_flat[:, :kv_width], span_window[:, :kv_width]], axis=0)
    all_values = jnp.concatenate([pool_flat[:, kv_width:], span_window[:, kv_width:]], axis=0)
    output = flash(
        queries,
        all_keys,
        all_values,
        row_group,
        row_start,
        row_last,
        key_tag,
        key_row,
        flags,
        Q_TILE,
        K_TILE,
        score_scale,
    )
    context = output.reshape(row_count, local_heads * HD)
    return (context, decode_cache)


def solution(mesh):
    dp_size, mp_size = mesh.devices.shape
    inner = Mesh(mesh.devices.reshape(dp_size // 2, 2, mp_size), ("dz", "dc", "mp"))
    dp = ("dz", "dc")
    return jax.shard_map(
        per_device,
        mesh=inner,
        in_specs=(
            P(dp, "mp"),
            P(),
            P(dp, "mp"),
            P(dp, "mp"),
            P(dp, "mp"),
            P("mp"),
            P("mp"),
            P("mp"),
            P(),
            P(),
            P(),
            P(),
            P(dp, None, "mp"),
            P(dp, None, "mp"),
            P(dp, None, None, None, "mp"),
            P(dp, None),
        ),
        out_specs=(P(dp, "mp"), P(dp, None, None, None, "mp")),
        check_vma=False,
    )
```

```python
import math

import jax
import jax.numpy as jnp
from jax import lax
from jax.sharding import Mesh, PartitionSpec as P

HD = 128
CAP = 2
MAX_REQUEST = 3072


NEG_BIG = -1e30
EPSILON = 1e-06
THETA = 1000000.0


def rotary(values, positions):
    head_dim = values.shape[-1]
    half_dim = head_dim // 2
    frequency = jnp.exp(
        -jnp.arange(half_dim, dtype=jnp.float32) * (2.0 / head_dim) * math.log(THETA)
    )
    angles = positions[:, None] * frequency[None, :]
    cosine = jnp.concatenate([jnp.cos(angles), jnp.cos(angles)], axis=-1)[:, None, :]
    sine_part = jnp.concatenate([jnp.sin(angles), jnp.sin(angles)], axis=-1)[:, None, :]
    first_half = values[..., :half_dim]
    second_half = values[..., half_dim:]
    turned = jnp.concatenate([-second_half, first_half], axis=-1)
    return values * cosine + turned * sine_part


def request_index(rows_here, ends_at):
    return jnp.sum((rows_here[:, None] >= ends_at[None, :]).astype(jnp.int32), axis=1)


def token_table(global_rows, request_lens, request_group, prompt_lens):
    ends_at = jnp.cumsum(request_lens)
    starts_at = ends_at - request_lens
    request_of = request_index(global_rows, ends_at)
    one_hot = request_of[:, None] == jnp.arange(request_lens.shape[0], dtype=jnp.int32)[None, :]
    first_row = jnp.sum(jnp.where(one_hot, starts_at[None, :], 0), axis=1)
    group_of = jnp.sum(jnp.where(one_hot, request_group[None, :], 0), axis=1)
    group_hot = group_of[:, None] == jnp.arange(prompt_lens.shape[0], dtype=jnp.int32)[None, :]
    prefix_of = jnp.sum(jnp.where(group_hot, prompt_lens[None, :], 0), axis=1)
    positions = (prefix_of + global_rows - first_row).astype(jnp.float32)
    return (request_of, group_hot, positions, ends_at)


def prompt_mask(prompt_table, prompt_lens, block_count, block_size):
    blocks = jnp.arange(block_count, dtype=jnp.int32)
    matching = prompt_table[:, :, None] == blocks[None, None, :]
    present = jnp.any(matching, axis=1)
    slot_no = jnp.sum(
        jnp.where(matching, jnp.arange(prompt_table.shape[1], dtype=jnp.int32)[None, :, None], 0),
        axis=1,
    )
    within = (
        slot_no[:, :, None] * block_size + jnp.arange(block_size, dtype=jnp.int32)[None, None, :]
    )
    allowed = present[:, :, None] & (within < prompt_lens[:, None, None])
    return allowed.reshape(prompt_table.shape[0], block_count * block_size)


def attend(current, queries, keys_flat, values_flat, allowed, score_scale):
    best_score, total_sum, accumulated = current
    scores = (
        jnp.einsum("kgqd,skd->kgqs", queries, keys_flat, preferred_element_type=jnp.float32)
        * score_scale
    )
    masked = allowed[None, None, :, :]
    scores = jnp.where(masked, scores, NEG_BIG)
    new_best = jnp.maximum(best_score, jnp.max(scores, axis=-1))
    weights = jnp.where(masked, jnp.exp(scores - new_best[..., None]), 0.0)
    factor = jnp.exp(best_score - new_best)
    total_sum = total_sum * factor + jnp.sum(weights, axis=-1)
    accumulated = accumulated * factor[..., None] + jnp.einsum(
        "kgqs,skd->kgqd",
        weights.astype(jnp.bfloat16),
        values_flat,
        preferred_element_type=jnp.float32,
    )
    return (new_best, total_sum, accumulated)


def dp_index():
    return lax.axis_index("dz") * lax.axis_size("dc") + lax.axis_index("dc")


def pack_cache(prev_cache, dest_device):
    blocks_here = prev_cache.shape[0]
    devices = lax.axis_size("dz") * lax.axis_size("dc")
    slot_count = devices * CAP
    target = dest_device[:, 0]
    same_target = target[:, None] == target[None, :]
    earlier = (
        jnp.arange(blocks_here, dtype=jnp.int32)[None, :]
        < jnp.arange(blocks_here, dtype=jnp.int32)[:, None]
    )
    block_rank = jnp.sum((same_target & earlier).astype(jnp.int32), axis=1)
    slot_device = jnp.arange(slot_count, dtype=jnp.int32) // CAP
    slot_rank = jnp.arange(slot_count, dtype=jnp.int32) % CAP
    matches = (target[None, :] == slot_device[:, None]) & (
        block_rank[None, :] == slot_rank[:, None]
    )
    filled = jnp.any(matches, axis=1)
    source = jnp.sum(
        jnp.where(matches, jnp.arange(blocks_here, dtype=jnp.int32)[None, :], 0), axis=1
    )
    packed = jnp.take(prev_cache, source, axis=0, mode="clip")
    slot_flags = filled.astype(jnp.bfloat16)
    return packed, slot_flags


def unpack_cache(packed, slot_flags):
    blocks_here = packed.shape[0] // CAP
    slot_count = packed.shape[0]
    arrived, arrived_flags = (
        lax.all_to_all(packed, ("dz", "dc"), split_axis=0, concat_axis=0, tiled=True),
        lax.all_to_all(slot_flags, ("dz", "dc"), split_axis=0, concat_axis=0, tiled=True),
    )
    arrived_live = arrived_flags > 0.5
    order_no = jnp.cumsum(arrived_live.astype(jnp.int32)) - 1
    picked = arrived_live[None, :] & (
        order_no[None, :] == jnp.arange(blocks_here, dtype=jnp.int32)[:, None]
    )
    chosen = jnp.sum(jnp.where(picked, jnp.arange(slot_count, dtype=jnp.int32)[None, :], 0), axis=1)
    return jnp.take(arrived, chosen, axis=0, mode="clip")


def per_device(
    hidden,
    norm_gain,
    query_weight,
    key_weight,
    value_weight,
    query_bias,
    key_bias,
    value_bias,
    request_lens,
    request_group,
    prompt_lens,
    prompt_table,
    pool_keys,
    pool_values,
    prev_cache,
    dest_device,
):
    row_count = hidden.shape[0]
    me = dp_index()
    side = lax.axis_index("dc")
    sides = lax.axis_size("dc")
    global_rows = me * row_count + jnp.arange(row_count, dtype=jnp.int32)
    request_of, group_hot, positions, ends_at = token_table(
        global_rows, request_lens, request_group, prompt_lens
    )
    mp_size = lax.axis_size("mp")
    spread = jnp.broadcast_to(hidden[None], (mp_size,) + hidden.shape)
    pieces = lax.all_to_all(spread, "mp", split_axis=0, concat_axis=0, tiled=True)
    packed, slot_flags = pack_cache(prev_cache, dest_device)
    pieces, packed, slot_flags = lax.optimization_barrier((pieces, packed, slot_flags))
    q_cols = query_weight.shape[1]
    k_cols = key_weight.shape[1]
    block_rows = query_weight.shape[0]
    pool_here = jnp.concatenate([pool_keys, pool_values], axis=2).reshape(block_rows, -1)
    weights_here = jnp.concatenate([query_weight, key_weight, value_weight, pool_here], axis=1)
    weights_all = lax.all_gather(weights_here, ("dz", "dc"), axis=0, tiled=True)
    proj_cols = q_cols + 2 * k_cols
    pool_all = weights_all[:, proj_cols:].reshape(
        (-1,) + pool_keys.shape[1:2] + (2 * pool_keys.shape[2],)
    )
    as_float = pieces.astype(jnp.float32)
    inverse = lax.rsqrt(
        jnp.mean(jnp.sum(as_float * as_float, axis=2), axis=0)[None, :, None] / pieces.shape[2]
        + EPSILON
    )
    gain = norm_gain.astype(jnp.float32).reshape(mp_size, 1, -1)
    normed = (as_float * inverse * gain).astype(jnp.bfloat16)
    proj = jnp.einsum(
        "jtf,jfc->tc",
        normed,
        weights_all.reshape(mp_size, -1, weights_all.shape[1]),
        preferred_element_type=jnp.float32,
    )
    query_proj = proj[:, :q_cols] + query_bias.astype(jnp.float32)[None, :]
    key_proj = proj[:, q_cols:q_cols + k_cols] + key_bias.astype(jnp.float32)[None, :]
    value_proj = proj[:, q_cols + k_cols:proj_cols] + value_bias.astype(jnp.float32)[None, :]
    local_heads = query_proj.shape[1] // HD
    local_kv = key_proj.shape[1] // HD
    group_size = local_heads // local_kv
    queries = rotary(query_proj.reshape(row_count, local_heads, HD), positions).astype(jnp.bfloat16)
    queries = queries.reshape(row_count, local_kv, group_size, HD).transpose(1, 2, 0, 3)
    keys_new = (
        rotary(key_proj.reshape(row_count, local_kv, HD), positions)
        .astype(jnp.bfloat16)
        .reshape(row_count, local_kv * HD)
    )
    values_new = value_proj.astype(jnp.bfloat16)
    span_here = jnp.concatenate([keys_new, values_new], axis=1)
    span_all = lax.all_gather(span_here, ("dz", "dc"), axis=0, tiled=True)
    packed, slot_flags, span_all = lax.optimization_barrier((packed, slot_flags, span_all))
    decode_cache = unpack_cache(packed, slot_flags)
    score_scale = HD ** (-0.5)
    carried = (
        jnp.full((local_kv, group_size, row_count), NEG_BIG, jnp.float32),
        jnp.zeros((local_kv, group_size, row_count), jnp.float32),
        jnp.zeros((local_kv, group_size, row_count, HD), jnp.float32),
    )
    block_size = pool_all.shape[1]
    blocks_here = pool_all.shape[0]
    kv_width = local_kv * HD
    allowed_group = prompt_mask(prompt_table, prompt_lens, blocks_here, block_size)
    allowed = jnp.any(group_hot[:, :, None] & allowed_group[None, :, :], axis=1)
    keys_flat = pool_all[:, :, :kv_width].reshape(blocks_here * block_size, local_kv, HD)
    values_flat = pool_all[:, :, kv_width:].reshape(blocks_here * block_size, local_kv, HD)
    carried = attend(carried, queries, keys_flat, values_flat, allowed, score_scale)
    key_count = span_all.shape[0]
    window = min(key_count, MAX_REQUEST + row_count)
    window = -(-window // row_count) * row_count
    window_start = jnp.maximum((me + 1) * row_count - window, 0)
    span_window = lax.dynamic_slice_in_dim(span_all, window_start, window, axis=0)
    key_rows = window_start + jnp.arange(window, dtype=jnp.int32)
    key_request = request_index(key_rows, ends_at)
    span_allowed = (request_of[:, None] == key_request[None, :]) & (
        key_rows[None, :] <= global_rows[:, None]
    )
    span_keys_flat = span_window[:, :kv_width].reshape(window, local_kv, HD)
    span_values_flat = span_window[:, kv_width:].reshape(window, local_kv, HD)
    carried = attend(
        carried, queries, span_keys_flat, span_values_flat, span_allowed, score_scale
    )
    best_score, total_sum, accumulated = carried
    output = accumulated / total_sum[..., None]
    context = output.transpose(2, 0, 1, 3).reshape(row_count, local_heads * HD).astype(jnp.bfloat16)
    return (context, decode_cache)


def solution(mesh):
    dp_size, mp_size = mesh.devices.shape
    inner = Mesh(mesh.devices.reshape(dp_size // 2, 2, mp_size), ("dz", "dc", "mp"))
    dp = ("dz", "dc")
    return jax.shard_map(
        per_device,
        mesh=inner,
        in_specs=(
            P(dp, "mp"),
            P(),
            P(dp, "mp"),
            P(dp, "mp"),
            P(dp, "mp"),
            P("mp"),
            P("mp"),
            P("mp"),
            P(),
            P(),
            P(),
            P(),
            P(dp, None, "mp"),
            P(dp, None, "mp"),
            P(dp, None, None, None, "mp"),
            P(dp, None),
        ),
        out_specs=(P(dp, "mp"), P(dp, None, None, None, "mp")),
        check_vma=False,
    )
```

```python
import math

import jax
import jax.numpy as jnp
from jax import lax
from jax.sharding import Mesh, PartitionSpec as P

HD = 128
CAP = 2
MAX_REQUEST = 3072


NEG_BIG = -1e30
EPSILON = 1e-06
THETA = 1000000.0


def rotary(values, positions):
    head_dim = values.shape[-1]
    half_dim = head_dim // 2
    frequency = jnp.exp(
        -jnp.arange(half_dim, dtype=jnp.float32) * (2.0 / head_dim) * math.log(THETA)
    )
    angles = positions[:, None] * frequency[None, :]
    cosine = jnp.concatenate([jnp.cos(angles), jnp.cos(angles)], axis=-1)[:, None, :]
    sine_part = jnp.concatenate([jnp.sin(angles), jnp.sin(angles)], axis=-1)[:, None, :]
    first_half = values[..., :half_dim]
    second_half = values[..., half_dim:]
    turned = jnp.concatenate([-second_half, first_half], axis=-1)
    return values * cosine + turned * sine_part


def request_index(rows_here, ends_at):
    return jnp.sum((rows_here[:, None] >= ends_at[None, :]).astype(jnp.int32), axis=1)


def token_table(global_rows, request_lens, request_group, prompt_lens):
    ends_at = jnp.cumsum(request_lens)
    starts_at = ends_at - request_lens
    request_of = request_index(global_rows, ends_at)
    one_hot = request_of[:, None] == jnp.arange(request_lens.shape[0], dtype=jnp.int32)[None, :]
    first_row = jnp.sum(jnp.where(one_hot, starts_at[None, :], 0), axis=1)
    group_of = jnp.sum(jnp.where(one_hot, request_group[None, :], 0), axis=1)
    group_hot = group_of[:, None] == jnp.arange(prompt_lens.shape[0], dtype=jnp.int32)[None, :]
    prefix_of = jnp.sum(jnp.where(group_hot, prompt_lens[None, :], 0), axis=1)
    positions = (prefix_of + global_rows - first_row).astype(jnp.float32)
    return (request_of, group_hot, positions, ends_at)


def prompt_mask(prompt_table, prompt_lens, block_count, block_size):
    blocks = jnp.arange(block_count, dtype=jnp.int32)
    matching = prompt_table[:, :, None] == blocks[None, None, :]
    present = jnp.any(matching, axis=1)
    slot_no = jnp.sum(
        jnp.where(matching, jnp.arange(prompt_table.shape[1], dtype=jnp.int32)[None, :, None], 0),
        axis=1,
    )
    within = (
        slot_no[:, :, None] * block_size + jnp.arange(block_size, dtype=jnp.int32)[None, None, :]
    )
    allowed = present[:, :, None] & (within < prompt_lens[:, None, None])
    return allowed.reshape(prompt_table.shape[0], block_count * block_size)


def attend(current, queries, keys_flat, values_flat, allowed, score_scale):
    best_score, total_sum, accumulated = current
    scores = (
        jnp.einsum("kgqd,skd->kgqs", queries, keys_flat, preferred_element_type=jnp.float32)
        * score_scale
    )
    masked = allowed[None, None, :, :]
    scores = jnp.where(masked, scores, NEG_BIG)
    new_best = jnp.maximum(best_score, jnp.max(scores, axis=-1))
    weights = jnp.where(masked, jnp.exp(scores - new_best[..., None]), 0.0)
    factor = jnp.exp(best_score - new_best)
    total_sum = total_sum * factor + jnp.sum(weights, axis=-1)
    accumulated = accumulated * factor[..., None] + jnp.einsum(
        "kgqs,skd->kgqd",
        weights.astype(jnp.bfloat16),
        values_flat,
        preferred_element_type=jnp.float32,
    )
    return (new_best, total_sum, accumulated)


def dp_index():
    return lax.axis_index("dz") * lax.axis_size("dc") + lax.axis_index("dc")


def pack_cache(prev_cache, dest_device):
    blocks_here = prev_cache.shape[0]
    devices = lax.axis_size("dz") * lax.axis_size("dc")
    slot_count = devices * CAP
    target = dest_device[:, 0]
    same_target = target[:, None] == target[None, :]
    earlier = (
        jnp.arange(blocks_here, dtype=jnp.int32)[None, :]
        < jnp.arange(blocks_here, dtype=jnp.int32)[:, None]
    )
    block_rank = jnp.sum((same_target & earlier).astype(jnp.int32), axis=1)
    slot_device = jnp.arange(slot_count, dtype=jnp.int32) // CAP
    slot_rank = jnp.arange(slot_count, dtype=jnp.int32) % CAP
    matches = (target[None, :] == slot_device[:, None]) & (
        block_rank[None, :] == slot_rank[:, None]
    )
    filled = jnp.any(matches, axis=1)
    source = jnp.sum(
        jnp.where(matches, jnp.arange(blocks_here, dtype=jnp.int32)[None, :], 0), axis=1
    )
    packed = jnp.take(prev_cache, source, axis=0, mode="clip")
    slot_flags = filled.astype(jnp.bfloat16)
    return packed, slot_flags


def swap_flags(slot_flags):
    return lax.all_to_all(slot_flags, ("dz", "dc"), split_axis=0, concat_axis=0, tiled=True)


def unpack_cache(packed, arrived_flags):
    blocks_here = packed.shape[0] // CAP
    slot_count = packed.shape[0]
    arrived = lax.all_to_all(packed, ("dz", "dc"), split_axis=0, concat_axis=0, tiled=True)
    arrived_live = arrived_flags > 0.5
    order_no = jnp.cumsum(arrived_live.astype(jnp.int32)) - 1
    picked = arrived_live[None, :] & (
        order_no[None, :] == jnp.arange(blocks_here, dtype=jnp.int32)[:, None]
    )
    chosen = jnp.sum(jnp.where(picked, jnp.arange(slot_count, dtype=jnp.int32)[None, :], 0), axis=1)
    return jnp.take(arrived, chosen, axis=0, mode="clip")


def per_device(
    hidden,
    norm_gain,
    query_weight,
    key_weight,
    value_weight,
    query_bias,
    key_bias,
    value_bias,
    request_lens,
    request_group,
    prompt_lens,
    prompt_table,
    pool_keys,
    pool_values,
    prev_cache,
    dest_device,
):
    row_count = hidden.shape[0]
    me = dp_index()
    side = lax.axis_index("dc")
    sides = lax.axis_size("dc")
    global_rows = me * row_count + jnp.arange(row_count, dtype=jnp.int32)
    request_of, group_hot, positions, ends_at = token_table(
        global_rows, request_lens, request_group, prompt_lens
    )
    mp_size = lax.axis_size("mp")
    spread = jnp.broadcast_to(hidden[None], (mp_size,) + hidden.shape)
    pieces = lax.all_to_all(spread, "mp", split_axis=0, concat_axis=0, tiled=True)
    packed, slot_flags = pack_cache(prev_cache, dest_device)
    pieces, packed, slot_flags = lax.optimization_barrier((pieces, packed, slot_flags))
    arrived_flags = swap_flags(slot_flags)
    q_cols = query_weight.shape[1]
    k_cols = key_weight.shape[1]
    block_rows = query_weight.shape[0]
    pool_here = jnp.concatenate([pool_keys, pool_values], axis=2).reshape(block_rows, -1)
    weights_here = jnp.concatenate([query_weight, key_weight, value_weight, pool_here], axis=1)
    weights_all = lax.all_gather(weights_here, ("dz", "dc"), axis=0, tiled=True)
    proj_cols = q_cols + 2 * k_cols
    pool_all = weights_all[:, proj_cols:].reshape(
        (-1,) + pool_keys.shape[1:2] + (2 * pool_keys.shape[2],)
    )
    as_float = pieces.astype(jnp.float32)
    inverse = lax.rsqrt(
        jnp.mean(jnp.sum(as_float * as_float, axis=2), axis=0)[None, :, None] / pieces.shape[2]
        + EPSILON
    )
    gain = norm_gain.astype(jnp.float32).reshape(mp_size, 1, -1)
    normed = (as_float * inverse * gain).astype(jnp.bfloat16)
    proj = jnp.einsum(
        "jtf,jfc->tc",
        normed,
        weights_all.reshape(mp_size, -1, weights_all.shape[1]),
        preferred_element_type=jnp.float32,
    )
    query_proj = proj[:, :q_cols] + query_bias.astype(jnp.float32)[None, :]
    key_proj = proj[:, q_cols:q_cols + k_cols] + key_bias.astype(jnp.float32)[None, :]
    value_proj = proj[:, q_cols + k_cols:proj_cols] + value_bias.astype(jnp.float32)[None, :]
    local_heads = query_proj.shape[1] // HD
    local_kv = key_proj.shape[1] // HD
    group_size = local_heads // local_kv
    queries = rotary(query_proj.reshape(row_count, local_heads, HD), positions).astype(jnp.bfloat16)
    queries = queries.reshape(row_count, local_kv, group_size, HD).transpose(1, 2, 0, 3)
    keys_new = (
        rotary(key_proj.reshape(row_count, local_kv, HD), positions)
        .astype(jnp.bfloat16)
        .reshape(row_count, local_kv * HD)
    )
    values_new = value_proj.astype(jnp.bfloat16)
    span_here = jnp.concatenate([keys_new, values_new], axis=1)
    span_all = lax.all_gather(span_here, ("dz", "dc"), axis=0, tiled=True)
    packed, arrived_flags, span_all = lax.optimization_barrier((packed, arrived_flags, span_all))
    decode_cache = unpack_cache(packed, arrived_flags)
    score_scale = HD ** (-0.5)
    carried = (
        jnp.full((local_kv, group_size, row_count), NEG_BIG, jnp.float32),
        jnp.zeros((local_kv, group_size, row_count), jnp.float32),
        jnp.zeros((local_kv, group_size, row_count, HD), jnp.float32),
    )
    block_size = pool_all.shape[1]
    blocks_here = pool_all.shape[0]
    kv_width = local_kv * HD
    allowed_group = prompt_mask(prompt_table, prompt_lens, blocks_here, block_size)
    allowed = jnp.any(group_hot[:, :, None] & allowed_group[None, :, :], axis=1)
    keys_flat = pool_all[:, :, :kv_width].reshape(blocks_here * block_size, local_kv, HD)
    values_flat = pool_all[:, :, kv_width:].reshape(blocks_here * block_size, local_kv, HD)
    carried = attend(carried, queries, keys_flat, values_flat, allowed, score_scale)
    key_count = span_all.shape[0]
    window = min(key_count, MAX_REQUEST + row_count)
    window = -(-window // row_count) * row_count
    window_start = jnp.maximum((me + 1) * row_count - window, 0)
    span_window = lax.dynamic_slice_in_dim(span_all, window_start, window, axis=0)
    key_rows = window_start + jnp.arange(window, dtype=jnp.int32)
    key_request = request_index(key_rows, ends_at)
    span_allowed = (request_of[:, None] == key_request[None, :]) & (
        key_rows[None, :] <= global_rows[:, None]
    )
    span_keys_flat = span_window[:, :kv_width].reshape(window, local_kv, HD)
    span_values_flat = span_window[:, kv_width:].reshape(window, local_kv, HD)
    carried = attend(
        carried, queries, span_keys_flat, span_values_flat, span_allowed, score_scale
    )
    best_score, total_sum, accumulated = carried
    output = accumulated / total_sum[..., None]
    context = output.transpose(2, 0, 1, 3).reshape(row_count, local_heads * HD).astype(jnp.bfloat16)
    return (context, decode_cache)


def solution(mesh):
    dp_size, mp_size = mesh.devices.shape
    inner = Mesh(mesh.devices.reshape(dp_size // 2, 2, mp_size), ("dz", "dc", "mp"))
    dp = ("dz", "dc")
    return jax.shard_map(
        per_device,
        mesh=inner,
        in_specs=(
            P(dp, "mp"),
            P(),
            P(dp, "mp"),
            P(dp, "mp"),
            P(dp, "mp"),
            P("mp"),
            P("mp"),
            P("mp"),
            P(),
            P(),
            P(),
            P(),
            P(dp, None, "mp"),
            P(dp, None, "mp"),
            P(dp, None, None, None, "mp"),
            P(dp, None),
        ),
        out_specs=(P(dp, "mp"), P(dp, None, None, None, "mp")),
        check_vma=False,
    )
```

```python
import math

import jax
import jax.numpy as jnp
from jax import lax
from jax.sharding import Mesh, PartitionSpec as P

HD = 128
CAP = 2
MAX_REQUEST = 3072


NEG_BIG = -1e30
EPSILON = 1e-06
THETA = 1000000.0


def rotary(values, positions):
    head_dim = values.shape[-1]
    half_dim = head_dim // 2
    frequency = jnp.exp(
        -jnp.arange(half_dim, dtype=jnp.float32) * (2.0 / head_dim) * math.log(THETA)
    )
    angles = positions[:, None] * frequency[None, :]
    cosine = jnp.concatenate([jnp.cos(angles), jnp.cos(angles)], axis=-1)[:, None, :]
    sine_part = jnp.concatenate([jnp.sin(angles), jnp.sin(angles)], axis=-1)[:, None, :]
    first_half = values[..., :half_dim]
    second_half = values[..., half_dim:]
    turned = jnp.concatenate([-second_half, first_half], axis=-1)
    return values * cosine + turned * sine_part


def request_index(rows_here, ends_at):
    return jnp.sum((rows_here[:, None] >= ends_at[None, :]).astype(jnp.int32), axis=1)


def token_table(global_rows, request_lens, request_group, prompt_lens):
    ends_at = jnp.cumsum(request_lens)
    starts_at = ends_at - request_lens
    request_of = request_index(global_rows, ends_at)
    one_hot = request_of[:, None] == jnp.arange(request_lens.shape[0], dtype=jnp.int32)[None, :]
    first_row = jnp.sum(jnp.where(one_hot, starts_at[None, :], 0), axis=1)
    group_of = jnp.sum(jnp.where(one_hot, request_group[None, :], 0), axis=1)
    group_hot = group_of[:, None] == jnp.arange(prompt_lens.shape[0], dtype=jnp.int32)[None, :]
    prefix_of = jnp.sum(jnp.where(group_hot, prompt_lens[None, :], 0), axis=1)
    positions = (prefix_of + global_rows - first_row).astype(jnp.float32)
    return (request_of, group_hot, positions, ends_at)


def prompt_mask(prompt_table, prompt_lens, block_count, block_size):
    blocks = jnp.arange(block_count, dtype=jnp.int32)
    matching = prompt_table[:, :, None] == blocks[None, None, :]
    present = jnp.any(matching, axis=1)
    slot_no = jnp.sum(
        jnp.where(matching, jnp.arange(prompt_table.shape[1], dtype=jnp.int32)[None, :, None], 0),
        axis=1,
    )
    within = (
        slot_no[:, :, None] * block_size + jnp.arange(block_size, dtype=jnp.int32)[None, None, :]
    )
    allowed = present[:, :, None] & (within < prompt_lens[:, None, None])
    return allowed.reshape(prompt_table.shape[0], block_count * block_size)


def attend(current, queries, keys_flat, values_flat, allowed, score_scale):
    best_score, total_sum, accumulated = current
    scores = (
        jnp.einsum("kgqd,skd->kgqs", queries, keys_flat, preferred_element_type=jnp.float32)
        * score_scale
    )
    masked = allowed[None, None, :, :]
    scores = jnp.where(masked, scores, NEG_BIG)
    new_best = jnp.maximum(best_score, jnp.max(scores, axis=-1))
    weights = jnp.where(masked, jnp.exp(scores - new_best[..., None]), 0.0)
    factor = jnp.exp(best_score - new_best)
    total_sum = total_sum * factor + jnp.sum(weights, axis=-1)
    accumulated = accumulated * factor[..., None] + jnp.einsum(
        "kgqs,skd->kgqd",
        weights.astype(jnp.bfloat16),
        values_flat,
        preferred_element_type=jnp.float32,
    )
    return (new_best, total_sum, accumulated)


def dp_index():
    return lax.axis_index("dz") * lax.axis_size("dc") + lax.axis_index("dc")


def pack_cache(prev_cache, dest_device):
    blocks_here = prev_cache.shape[0]
    devices = lax.axis_size("dz") * lax.axis_size("dc")
    slot_count = devices * CAP
    target = dest_device[:, 0]
    same_target = target[:, None] == target[None, :]
    earlier = (
        jnp.arange(blocks_here, dtype=jnp.int32)[None, :]
        < jnp.arange(blocks_here, dtype=jnp.int32)[:, None]
    )
    block_rank = jnp.sum((same_target & earlier).astype(jnp.int32), axis=1)
    slot_device = jnp.arange(slot_count, dtype=jnp.int32) // CAP
    slot_rank = jnp.arange(slot_count, dtype=jnp.int32) % CAP
    matches = (target[None, :] == slot_device[:, None]) & (
        block_rank[None, :] == slot_rank[:, None]
    )
    filled = jnp.any(matches, axis=1)
    source = jnp.sum(
        jnp.where(matches, jnp.arange(blocks_here, dtype=jnp.int32)[None, :], 0), axis=1
    )
    packed = jnp.take(prev_cache, source, axis=0, mode="clip")
    slot_flags = filled.astype(jnp.bfloat16)
    return packed, slot_flags


def swap_flags(slot_flags):
    return lax.all_to_all(slot_flags, ("dz", "dc"), split_axis=0, concat_axis=0, tiled=True)


def unpack_cache(packed, arrived_flags):
    blocks_here = packed.shape[0] // CAP
    slot_count = packed.shape[0]
    arrived = lax.all_to_all(packed, ("dz", "dc"), split_axis=0, concat_axis=0, tiled=True)
    arrived_live = arrived_flags > 0.5
    order_no = jnp.cumsum(arrived_live.astype(jnp.int32)) - 1
    picked = arrived_live[None, :] & (
        order_no[None, :] == jnp.arange(blocks_here, dtype=jnp.int32)[:, None]
    )
    chosen = jnp.sum(jnp.where(picked, jnp.arange(slot_count, dtype=jnp.int32)[None, :], 0), axis=1)
    return jnp.take(arrived, chosen, axis=0, mode="clip")


def per_device(
    hidden,
    norm_gain,
    query_weight,
    key_weight,
    value_weight,
    query_bias,
    key_bias,
    value_bias,
    request_lens,
    request_group,
    prompt_lens,
    prompt_table,
    pool_keys,
    pool_values,
    prev_cache,
    dest_device,
):
    row_count = hidden.shape[0]
    me = dp_index()
    side = lax.axis_index("dc")
    sides = lax.axis_size("dc")
    global_rows = me * row_count + jnp.arange(row_count, dtype=jnp.int32)
    request_of, group_hot, positions, ends_at = token_table(
        global_rows, request_lens, request_group, prompt_lens
    )
    mp_size = lax.axis_size("mp")
    spread = jnp.broadcast_to(hidden[None], (mp_size,) + hidden.shape)
    pieces = lax.all_to_all(spread, "mp", split_axis=0, concat_axis=0, tiled=True)
    packed, slot_flags = pack_cache(prev_cache, dest_device)
    arrived_flags = swap_flags(slot_flags)
    pieces, packed, arrived_flags = lax.optimization_barrier((pieces, packed, arrived_flags))
    q_cols = query_weight.shape[1]
    k_cols = key_weight.shape[1]
    block_rows = query_weight.shape[0]
    pool_here = jnp.concatenate([pool_keys, pool_values], axis=2).reshape(block_rows, -1)
    weights_here = jnp.concatenate([query_weight, key_weight, value_weight, pool_here], axis=1)
    weights_all = lax.all_gather(weights_here, ("dz", "dc"), axis=0, tiled=True)
    proj_cols = q_cols + 2 * k_cols
    pool_all = weights_all[:, proj_cols:].reshape(
        (-1,) + pool_keys.shape[1:2] + (2 * pool_keys.shape[2],)
    )
    as_float = pieces.astype(jnp.float32)
    inverse = lax.rsqrt(
        jnp.mean(jnp.sum(as_float * as_float, axis=2), axis=0)[None, :, None] / pieces.shape[2]
        + EPSILON
    )
    gain = norm_gain.astype(jnp.float32).reshape(mp_size, 1, -1)
    normed = (as_float * inverse * gain).astype(jnp.bfloat16)
    proj = jnp.einsum(
        "jtf,jfc->tc",
        normed,
        weights_all.reshape(mp_size, -1, weights_all.shape[1]),
        preferred_element_type=jnp.float32,
    )
    query_proj = proj[:, :q_cols] + query_bias.astype(jnp.float32)[None, :]
    key_proj = proj[:, q_cols:q_cols + k_cols] + key_bias.astype(jnp.float32)[None, :]
    value_proj = proj[:, q_cols + k_cols:proj_cols] + value_bias.astype(jnp.float32)[None, :]
    local_heads = query_proj.shape[1] // HD
    local_kv = key_proj.shape[1] // HD
    group_size = local_heads // local_kv
    queries = rotary(query_proj.reshape(row_count, local_heads, HD), positions).astype(jnp.bfloat16)
    queries = queries.reshape(row_count, local_kv, group_size, HD).transpose(1, 2, 0, 3)
    keys_new = (
        rotary(key_proj.reshape(row_count, local_kv, HD), positions)
        .astype(jnp.bfloat16)
        .reshape(row_count, local_kv * HD)
    )
    values_new = value_proj.astype(jnp.bfloat16)
    span_here = jnp.concatenate([keys_new, values_new], axis=1)
    span_all = lax.all_gather(span_here, ("dz", "dc"), axis=0, tiled=True)
    packed, arrived_flags, span_all = lax.optimization_barrier((packed, arrived_flags, span_all))
    decode_cache = unpack_cache(packed, arrived_flags)
    score_scale = HD ** (-0.5)
    carried = (
        jnp.full((local_kv, group_size, row_count), NEG_BIG, jnp.float32),
        jnp.zeros((local_kv, group_size, row_count), jnp.float32),
        jnp.zeros((local_kv, group_size, row_count, HD), jnp.float32),
    )
    block_size = pool_all.shape[1]
    blocks_here = pool_all.shape[0]
    kv_width = local_kv * HD
    allowed_group = prompt_mask(prompt_table, prompt_lens, blocks_here, block_size)
    allowed = jnp.any(group_hot[:, :, None] & allowed_group[None, :, :], axis=1)
    keys_flat = pool_all[:, :, :kv_width].reshape(blocks_here * block_size, local_kv, HD)
    values_flat = pool_all[:, :, kv_width:].reshape(blocks_here * block_size, local_kv, HD)
    carried = attend(carried, queries, keys_flat, values_flat, allowed, score_scale)
    key_count = span_all.shape[0]
    window = min(key_count, MAX_REQUEST + row_count)
    window = -(-window // row_count) * row_count
    window_start = jnp.maximum((me + 1) * row_count - window, 0)
    span_window = lax.dynamic_slice_in_dim(span_all, window_start, window, axis=0)
    key_rows = window_start + jnp.arange(window, dtype=jnp.int32)
    key_request = request_index(key_rows, ends_at)
    span_allowed = (request_of[:, None] == key_request[None, :]) & (
        key_rows[None, :] <= global_rows[:, None]
    )
    span_keys_flat = span_window[:, :kv_width].reshape(window, local_kv, HD)
    span_values_flat = span_window[:, kv_width:].reshape(window, local_kv, HD)
    carried = attend(
        carried, queries, span_keys_flat, span_values_flat, span_allowed, score_scale
    )
    best_score, total_sum, accumulated = carried
    output = accumulated / total_sum[..., None]
    context = output.transpose(2, 0, 1, 3).reshape(row_count, local_heads * HD).astype(jnp.bfloat16)
    return (context, decode_cache)


def solution(mesh):
    dp_size, mp_size = mesh.devices.shape
    inner = Mesh(mesh.devices.reshape(dp_size // 2, 2, mp_size), ("dz", "dc", "mp"))
    dp = ("dz", "dc")
    return jax.shard_map(
        per_device,
        mesh=inner,
        in_specs=(
            P(dp, "mp"),
            P(),
            P(dp, "mp"),
            P(dp, "mp"),
            P(dp, "mp"),
            P("mp"),
            P("mp"),
            P("mp"),
            P(),
            P(),
            P(),
            P(),
            P(dp, None, "mp"),
            P(dp, None, "mp"),
            P(dp, None, None, None, "mp"),
            P(dp, None),
        ),
        out_specs=(P(dp, "mp"), P(dp, None, None, None, "mp")),
        check_vma=False,
    )
```

```python
import math

import jax
import jax.numpy as jnp
from jax import lax
from jax.sharding import Mesh, PartitionSpec as P

HD = 128
CAP = 2
MAX_REQUEST = 3072


NEG_BIG = -1e30
EPSILON = 1e-06
THETA = 1000000.0


def rotary(values, positions):
    head_dim = values.shape[-1]
    half_dim = head_dim // 2
    frequency = jnp.exp(
        -jnp.arange(half_dim, dtype=jnp.float32) * (2.0 / head_dim) * math.log(THETA)
    )
    angles = positions[:, None] * frequency[None, :]
    cosine = jnp.concatenate([jnp.cos(angles), jnp.cos(angles)], axis=-1)[:, None, :]
    sine_part = jnp.concatenate([jnp.sin(angles), jnp.sin(angles)], axis=-1)[:, None, :]
    first_half = values[..., :half_dim]
    second_half = values[..., half_dim:]
    turned = jnp.concatenate([-second_half, first_half], axis=-1)
    return values * cosine + turned * sine_part


def request_index(rows_here, ends_at):
    return jnp.sum((rows_here[:, None] >= ends_at[None, :]).astype(jnp.int32), axis=1)


def token_table(global_rows, request_lens, request_group, prompt_lens):
    ends_at = jnp.cumsum(request_lens)
    starts_at = ends_at - request_lens
    request_of = request_index(global_rows, ends_at)
    one_hot = request_of[:, None] == jnp.arange(request_lens.shape[0], dtype=jnp.int32)[None, :]
    first_row = jnp.sum(jnp.where(one_hot, starts_at[None, :], 0), axis=1)
    group_of = jnp.sum(jnp.where(one_hot, request_group[None, :], 0), axis=1)
    group_hot = group_of[:, None] == jnp.arange(prompt_lens.shape[0], dtype=jnp.int32)[None, :]
    prefix_of = jnp.sum(jnp.where(group_hot, prompt_lens[None, :], 0), axis=1)
    positions = (prefix_of + global_rows - first_row).astype(jnp.float32)
    return (request_of, group_hot, positions, ends_at)


def prompt_mask(prompt_table, prompt_lens, block_count, block_size):
    blocks = jnp.arange(block_count, dtype=jnp.int32)
    matching = prompt_table[:, :, None] == blocks[None, None, :]
    present = jnp.any(matching, axis=1)
    slot_no = jnp.sum(
        jnp.where(matching, jnp.arange(prompt_table.shape[1], dtype=jnp.int32)[None, :, None], 0),
        axis=1,
    )
    within = (
        slot_no[:, :, None] * block_size + jnp.arange(block_size, dtype=jnp.int32)[None, None, :]
    )
    allowed = present[:, :, None] & (within < prompt_lens[:, None, None])
    return allowed.reshape(prompt_table.shape[0], block_count * block_size)


def attend(current, queries, keys_flat, values_flat, allowed, score_scale):
    best_score, total_sum, accumulated = current
    scores = (
        jnp.einsum("kgqd,skd->kgqs", queries, keys_flat, preferred_element_type=jnp.float32)
        * score_scale
    )
    masked = allowed[None, None, :, :]
    scores = jnp.where(masked, scores, NEG_BIG)
    new_best = jnp.maximum(best_score, jnp.max(scores, axis=-1))
    weights = jnp.where(masked, jnp.exp(scores - new_best[..., None]), 0.0)
    factor = jnp.exp(best_score - new_best)
    total_sum = total_sum * factor + jnp.sum(weights, axis=-1)
    accumulated = accumulated * factor[..., None] + jnp.einsum(
        "kgqs,skd->kgqd",
        weights.astype(jnp.bfloat16),
        values_flat,
        preferred_element_type=jnp.float32,
    )
    return (new_best, total_sum, accumulated)


def dp_index():
    return lax.axis_index("dz") * lax.axis_size("dc") + lax.axis_index("dc")


def pack_cache(prev_cache, dest_device):
    blocks_here = prev_cache.shape[0]
    devices = lax.axis_size("dz") * lax.axis_size("dc")
    slot_count = devices * CAP
    target = dest_device[:, 0]
    same_target = target[:, None] == target[None, :]
    earlier = (
        jnp.arange(blocks_here, dtype=jnp.int32)[None, :]
        < jnp.arange(blocks_here, dtype=jnp.int32)[:, None]
    )
    block_rank = jnp.sum((same_target & earlier).astype(jnp.int32), axis=1)
    slot_device = jnp.arange(slot_count, dtype=jnp.int32) // CAP
    slot_rank = jnp.arange(slot_count, dtype=jnp.int32) % CAP
    matches = (target[None, :] == slot_device[:, None]) & (
        block_rank[None, :] == slot_rank[:, None]
    )
    filled = jnp.any(matches, axis=1)
    source = jnp.sum(
        jnp.where(matches, jnp.arange(blocks_here, dtype=jnp.int32)[None, :], 0), axis=1
    )
    packed = jnp.take(prev_cache, source, axis=0, mode="clip")
    slot_flags = filled.astype(jnp.bfloat16)
    return packed, slot_flags


def swap_flags(slot_flags):
    return lax.all_to_all(slot_flags, ("dz", "dc"), split_axis=0, concat_axis=0, tiled=True)


def unpack_cache(packed, arrived_flags):
    blocks_here = packed.shape[0] // CAP
    slot_count = packed.shape[0]
    arrived = lax.all_to_all(packed, ("dz", "dc"), split_axis=0, concat_axis=0, tiled=True)
    arrived_live = arrived_flags > 0.5
    order_no = jnp.cumsum(arrived_live.astype(jnp.int32)) - 1
    picked = arrived_live[None, :] & (
        order_no[None, :] == jnp.arange(blocks_here, dtype=jnp.int32)[:, None]
    )
    chosen = jnp.sum(jnp.where(picked, jnp.arange(slot_count, dtype=jnp.int32)[None, :], 0), axis=1)
    return jnp.take(arrived, chosen, axis=0, mode="clip")


def per_device(
    hidden,
    norm_gain,
    query_weight,
    key_weight,
    value_weight,
    query_bias,
    key_bias,
    value_bias,
    request_lens,
    request_group,
    prompt_lens,
    prompt_table,
    pool_keys,
    pool_values,
    prev_cache,
    dest_device,
):
    row_count = hidden.shape[0]
    me = dp_index()
    side = lax.axis_index("dc")
    sides = lax.axis_size("dc")
    global_rows = me * row_count + jnp.arange(row_count, dtype=jnp.int32)
    request_of, group_hot, positions, ends_at = token_table(
        global_rows, request_lens, request_group, prompt_lens
    )
    mp_size = lax.axis_size("mp")
    spread = jnp.broadcast_to(hidden[None], (mp_size,) + hidden.shape)
    pieces = lax.all_to_all(spread, "mp", split_axis=0, concat_axis=0, tiled=True)
    packed, slot_flags = pack_cache(prev_cache, dest_device)
    arrived_flags = swap_flags(slot_flags)
    all_blocks = pool_keys.shape[0] * lax.axis_size("dz") * lax.axis_size("dc")
    allowed_group = prompt_mask(prompt_table, prompt_lens, all_blocks, pool_keys.shape[1])
    allowed = jnp.any(group_hot[:, :, None] & allowed_group[None, :, :], axis=1)
    key_count = row_count * lax.axis_size("dz") * lax.axis_size("dc")
    window = min(key_count, MAX_REQUEST + row_count)
    window = -(-window // row_count) * row_count
    window_start = jnp.maximum((me + 1) * row_count - window, 0)
    key_rows = window_start + jnp.arange(window, dtype=jnp.int32)
    key_request = request_index(key_rows, ends_at)
    span_allowed = (request_of[:, None] == key_request[None, :]) & (
        key_rows[None, :] <= global_rows[:, None]
    )
    pieces, packed, arrived_flags, allowed, span_allowed = lax.optimization_barrier(
        (pieces, packed, arrived_flags, allowed, span_allowed)
    )
    q_cols = query_weight.shape[1]
    k_cols = key_weight.shape[1]
    block_rows = query_weight.shape[0]
    pool_here = jnp.concatenate([pool_keys, pool_values], axis=2).reshape(block_rows, -1)
    weights_here = jnp.concatenate([query_weight, key_weight, value_weight, pool_here], axis=1)
    weights_all = lax.all_gather(weights_here, ("dz", "dc"), axis=0, tiled=True)
    proj_cols = q_cols + 2 * k_cols
    pool_all = weights_all[:, proj_cols:].reshape(
        (-1,) + pool_keys.shape[1:2] + (2 * pool_keys.shape[2],)
    )
    as_float = pieces.astype(jnp.float32)
    inverse = lax.rsqrt(
        jnp.mean(jnp.sum(as_float * as_float, axis=2), axis=0)[None, :, None] / pieces.shape[2]
        + EPSILON
    )
    gain = norm_gain.astype(jnp.float32).reshape(mp_size, 1, -1)
    normed = (as_float * inverse * gain).astype(jnp.bfloat16)
    proj = jnp.einsum(
        "jtf,jfc->tc",
        normed,
        weights_all.reshape(mp_size, -1, weights_all.shape[1]),
        preferred_element_type=jnp.float32,
    )
    query_proj = proj[:, :q_cols] + query_bias.astype(jnp.float32)[None, :]
    key_proj = proj[:, q_cols:q_cols + k_cols] + key_bias.astype(jnp.float32)[None, :]
    value_proj = proj[:, q_cols + k_cols:proj_cols] + value_bias.astype(jnp.float32)[None, :]
    local_heads = query_proj.shape[1] // HD
    local_kv = key_proj.shape[1] // HD
    group_size = local_heads // local_kv
    queries = rotary(query_proj.reshape(row_count, local_heads, HD), positions).astype(jnp.bfloat16)
    queries = queries.reshape(row_count, local_kv, group_size, HD).transpose(1, 2, 0, 3)
    keys_new = (
        rotary(key_proj.reshape(row_count, local_kv, HD), positions)
        .astype(jnp.bfloat16)
        .reshape(row_count, local_kv * HD)
    )
    values_new = value_proj.astype(jnp.bfloat16)
    span_here = jnp.concatenate([keys_new, values_new], axis=1)
    span_all = lax.all_gather(span_here, ("dz", "dc"), axis=0, tiled=True)
    packed, arrived_flags, span_all = lax.optimization_barrier((packed, arrived_flags, span_all))
    decode_cache = unpack_cache(packed, arrived_flags)
    score_scale = HD ** (-0.5)
    carried = (
        jnp.full((local_kv, group_size, row_count), NEG_BIG, jnp.float32),
        jnp.zeros((local_kv, group_size, row_count), jnp.float32),
        jnp.zeros((local_kv, group_size, row_count, HD), jnp.float32),
    )
    block_size = pool_all.shape[1]
    blocks_here = pool_all.shape[0]
    kv_width = local_kv * HD
    keys_flat = pool_all[:, :, :kv_width].reshape(blocks_here * block_size, local_kv, HD)
    values_flat = pool_all[:, :, kv_width:].reshape(blocks_here * block_size, local_kv, HD)
    carried = attend(carried, queries, keys_flat, values_flat, allowed, score_scale)
    key_count = span_all.shape[0]
    span_window = lax.dynamic_slice_in_dim(span_all, window_start, window, axis=0)
    span_keys_flat = span_window[:, :kv_width].reshape(window, local_kv, HD)
    span_values_flat = span_window[:, kv_width:].reshape(window, local_kv, HD)
    carried = attend(
        carried, queries, span_keys_flat, span_values_flat, span_allowed, score_scale
    )
    best_score, total_sum, accumulated = carried
    output = accumulated / total_sum[..., None]
    context = output.transpose(2, 0, 1, 3).reshape(row_count, local_heads * HD).astype(jnp.bfloat16)
    return (context, decode_cache)


def solution(mesh):
    dp_size, mp_size = mesh.devices.shape
    inner = Mesh(mesh.devices.reshape(dp_size // 2, 2, mp_size), ("dz", "dc", "mp"))
    dp = ("dz", "dc")
    return jax.shard_map(
        per_device,
        mesh=inner,
        in_specs=(
            P(dp, "mp"),
            P(),
            P(dp, "mp"),
            P(dp, "mp"),
            P(dp, "mp"),
            P("mp"),
            P("mp"),
            P("mp"),
            P(),
            P(),
            P(),
            P(),
            P(dp, None, "mp"),
            P(dp, None, "mp"),
            P(dp, None, None, None, "mp"),
            P(dp, None),
        ),
        out_specs=(P(dp, "mp"), P(dp, None, None, None, "mp")),
        check_vma=False,
    )
```

```python
import math

import jax
import jax.numpy as jnp
from jax import lax
from jax.sharding import Mesh, PartitionSpec as P

HD = 128
CAP = 2
MAX_REQUEST = 3072


NEG_BIG = -1e30
EPSILON = 1e-06
THETA = 1000000.0


def rotary(values, positions):
    head_dim = values.shape[-1]
    half_dim = head_dim // 2
    frequency = jnp.exp(
        -jnp.arange(half_dim, dtype=jnp.float32) * (2.0 / head_dim) * math.log(THETA)
    )
    angles = positions[:, None] * frequency[None, :]
    cosine = jnp.concatenate([jnp.cos(angles), jnp.cos(angles)], axis=-1)[:, None, :]
    sine_part = jnp.concatenate([jnp.sin(angles), jnp.sin(angles)], axis=-1)[:, None, :]
    first_half = values[..., :half_dim]
    second_half = values[..., half_dim:]
    turned = jnp.concatenate([-second_half, first_half], axis=-1)
    return values * cosine + turned * sine_part


def request_index(rows_here, ends_at):
    return jnp.sum((rows_here[:, None] >= ends_at[None, :]).astype(jnp.int32), axis=1)


def token_table(global_rows, request_lens, request_group, prompt_lens):
    ends_at = jnp.cumsum(request_lens)
    starts_at = ends_at - request_lens
    request_of = request_index(global_rows, ends_at)
    one_hot = request_of[:, None] == jnp.arange(request_lens.shape[0], dtype=jnp.int32)[None, :]
    first_row = jnp.sum(jnp.where(one_hot, starts_at[None, :], 0), axis=1)
    group_of = jnp.sum(jnp.where(one_hot, request_group[None, :], 0), axis=1)
    group_hot = group_of[:, None] == jnp.arange(prompt_lens.shape[0], dtype=jnp.int32)[None, :]
    prefix_of = jnp.sum(jnp.where(group_hot, prompt_lens[None, :], 0), axis=1)
    positions = (prefix_of + global_rows - first_row).astype(jnp.float32)
    return (request_of, group_hot, positions, ends_at)


def prompt_mask(prompt_table, prompt_lens, block_count, block_size):
    blocks = jnp.arange(block_count, dtype=jnp.int32)
    matching = prompt_table[:, :, None] == blocks[None, None, :]
    present = jnp.any(matching, axis=1)
    slot_no = jnp.sum(
        jnp.where(matching, jnp.arange(prompt_table.shape[1], dtype=jnp.int32)[None, :, None], 0),
        axis=1,
    )
    within = (
        slot_no[:, :, None] * block_size + jnp.arange(block_size, dtype=jnp.int32)[None, None, :]
    )
    allowed = present[:, :, None] & (within < prompt_lens[:, None, None])
    return allowed.reshape(prompt_table.shape[0], block_count * block_size)


def attend(current, queries, keys_flat, values_flat, allowed, score_scale):
    best_score, total_sum, accumulated = current
    scores = (
        jnp.einsum("kgqd,skd->kgqs", queries, keys_flat, preferred_element_type=jnp.float32)
        * score_scale
    )
    masked = allowed[None, None, :, :]
    scores = jnp.where(masked, scores, NEG_BIG)
    new_best = jnp.maximum(best_score, jnp.max(scores, axis=-1))
    weights = jnp.where(masked, jnp.exp(scores - new_best[..., None]), 0.0)
    factor = jnp.exp(best_score - new_best)
    total_sum = total_sum * factor + jnp.sum(weights, axis=-1)
    accumulated = accumulated * factor[..., None] + jnp.einsum(
        "kgqs,skd->kgqd",
        weights.astype(jnp.bfloat16),
        values_flat,
        preferred_element_type=jnp.float32,
    )
    return (new_best, total_sum, accumulated)


def dp_index():
    return lax.axis_index("dz") * lax.axis_size("dc") + lax.axis_index("dc")


def pack_cache(prev_cache, dest_device):
    blocks_here = prev_cache.shape[0]
    devices = lax.axis_size("dz") * lax.axis_size("dc")
    slot_count = devices * CAP
    target = dest_device[:, 0]
    same_target = target[:, None] == target[None, :]
    earlier = (
        jnp.arange(blocks_here, dtype=jnp.int32)[None, :]
        < jnp.arange(blocks_here, dtype=jnp.int32)[:, None]
    )
    block_rank = jnp.sum((same_target & earlier).astype(jnp.int32), axis=1)
    slot_device = jnp.arange(slot_count, dtype=jnp.int32) // CAP
    slot_rank = jnp.arange(slot_count, dtype=jnp.int32) % CAP
    matches = (target[None, :] == slot_device[:, None]) & (
        block_rank[None, :] == slot_rank[:, None]
    )
    filled = jnp.any(matches, axis=1)
    source = jnp.sum(
        jnp.where(matches, jnp.arange(blocks_here, dtype=jnp.int32)[None, :], 0), axis=1
    )
    packed = jnp.take(prev_cache, source, axis=0, mode="clip")
    slot_flags = filled.astype(jnp.bfloat16)
    return packed, slot_flags


def swap_flags(slot_flags):
    return lax.all_to_all(slot_flags, ("dz", "dc"), split_axis=0, concat_axis=0, tiled=True)


def unpack_cache(packed, arrived_flags):
    blocks_here = packed.shape[0] // CAP
    slot_count = packed.shape[0]
    arrived = lax.all_to_all(packed, ("dz", "dc"), split_axis=0, concat_axis=0, tiled=True)
    arrived_live = arrived_flags > 0.5
    order_no = jnp.cumsum(arrived_live.astype(jnp.int32)) - 1
    picked = arrived_live[None, :] & (
        order_no[None, :] == jnp.arange(blocks_here, dtype=jnp.int32)[:, None]
    )
    chosen = jnp.sum(jnp.where(picked, jnp.arange(slot_count, dtype=jnp.int32)[None, :], 0), axis=1)
    return jnp.take(arrived, chosen, axis=0, mode="clip")


def per_device(
    hidden,
    norm_gain,
    query_weight,
    key_weight,
    value_weight,
    query_bias,
    key_bias,
    value_bias,
    request_lens,
    request_group,
    prompt_lens,
    prompt_table,
    pool_keys,
    pool_values,
    prev_cache,
    dest_device,
):
    row_count = hidden.shape[0]
    me = dp_index()
    side = lax.axis_index("dc")
    sides = lax.axis_size("dc")
    global_rows = me * row_count + jnp.arange(row_count, dtype=jnp.int32)
    request_of, group_hot, positions, ends_at = token_table(
        global_rows, request_lens, request_group, prompt_lens
    )
    mp_size = lax.axis_size("mp")
    spread = jnp.broadcast_to(hidden[None], (mp_size,) + hidden.shape)
    pieces = lax.all_to_all(spread, "mp", split_axis=0, concat_axis=0, tiled=True)
    packed, slot_flags = pack_cache(prev_cache, dest_device)
    arrived_flags = swap_flags(slot_flags)
    pieces, packed, arrived_flags = lax.optimization_barrier((pieces, packed, arrived_flags))
    q_cols = query_weight.shape[1]
    k_cols = key_weight.shape[1]
    block_rows = query_weight.shape[0]
    pool_here = jnp.concatenate([pool_keys, pool_values], axis=2).reshape(block_rows, -1)
    weights_here = jnp.concatenate([query_weight, key_weight, value_weight, pool_here], axis=1)
    weights_all = lax.all_gather(weights_here, ("dz", "dc"), axis=0, tiled=True)
    proj_cols = q_cols + 2 * k_cols
    pool_all = weights_all[:, proj_cols:].reshape(
        (-1,) + pool_keys.shape[1:2] + (2 * pool_keys.shape[2],)
    )
    as_float = pieces.astype(jnp.float32)
    inverse = lax.rsqrt(
        jnp.mean(jnp.sum(as_float * as_float, axis=2), axis=0)[None, :, None] / pieces.shape[2]
        + EPSILON
    )
    gain = norm_gain.astype(jnp.float32).reshape(mp_size, 1, -1)
    normed = (as_float * inverse * gain).astype(jnp.bfloat16)
    normed = lax.optimization_barrier(normed)
    proj = jnp.einsum(
        "jtf,jfc->tc",
        normed,
        weights_all.reshape(mp_size, -1, weights_all.shape[1]),
        preferred_element_type=jnp.float32,
    )
    query_proj = proj[:, :q_cols] + query_bias.astype(jnp.float32)[None, :]
    key_proj = proj[:, q_cols:q_cols + k_cols] + key_bias.astype(jnp.float32)[None, :]
    value_proj = proj[:, q_cols + k_cols:proj_cols] + value_bias.astype(jnp.float32)[None, :]
    local_heads = query_proj.shape[1] // HD
    local_kv = key_proj.shape[1] // HD
    group_size = local_heads // local_kv
    queries = rotary(query_proj.reshape(row_count, local_heads, HD), positions).astype(jnp.bfloat16)
    queries = queries.reshape(row_count, local_kv, group_size, HD).transpose(1, 2, 0, 3)
    keys_new = (
        rotary(key_proj.reshape(row_count, local_kv, HD), positions)
        .astype(jnp.bfloat16)
        .reshape(row_count, local_kv * HD)
    )
    values_new = value_proj.astype(jnp.bfloat16)
    span_here = jnp.concatenate([keys_new, values_new], axis=1)
    span_all = lax.all_gather(span_here, ("dz", "dc"), axis=0, tiled=True)
    packed, arrived_flags, span_all = lax.optimization_barrier((packed, arrived_flags, span_all))
    decode_cache = unpack_cache(packed, arrived_flags)
    score_scale = HD ** (-0.5)
    carried = (
        jnp.full((local_kv, group_size, row_count), NEG_BIG, jnp.float32),
        jnp.zeros((local_kv, group_size, row_count), jnp.float32),
        jnp.zeros((local_kv, group_size, row_count, HD), jnp.float32),
    )
    block_size = pool_all.shape[1]
    blocks_here = pool_all.shape[0]
    kv_width = local_kv * HD
    allowed_group = prompt_mask(prompt_table, prompt_lens, blocks_here, block_size)
    allowed = jnp.any(group_hot[:, :, None] & allowed_group[None, :, :], axis=1)
    keys_flat = pool_all[:, :, :kv_width].reshape(blocks_here * block_size, local_kv, HD)
    values_flat = pool_all[:, :, kv_width:].reshape(blocks_here * block_size, local_kv, HD)
    carried = attend(carried, queries, keys_flat, values_flat, allowed, score_scale)
    key_count = span_all.shape[0]
    window = min(key_count, MAX_REQUEST + row_count)
    window = -(-window // row_count) * row_count
    window_start = jnp.maximum((me + 1) * row_count - window, 0)
    span_window = lax.dynamic_slice_in_dim(span_all, window_start, window, axis=0)
    key_rows = window_start + jnp.arange(window, dtype=jnp.int32)
    key_request = request_index(key_rows, ends_at)
    span_allowed = (request_of[:, None] == key_request[None, :]) & (
        key_rows[None, :] <= global_rows[:, None]
    )
    span_keys_flat = span_window[:, :kv_width].reshape(window, local_kv, HD)
    span_values_flat = span_window[:, kv_width:].reshape(window, local_kv, HD)
    carried = attend(
        carried, queries, span_keys_flat, span_values_flat, span_allowed, score_scale
    )
    best_score, total_sum, accumulated = carried
    output = accumulated / total_sum[..., None]
    context = output.transpose(2, 0, 1, 3).reshape(row_count, local_heads * HD).astype(jnp.bfloat16)
    return (context, decode_cache)


def solution(mesh):
    dp_size, mp_size = mesh.devices.shape
    inner = Mesh(mesh.devices.reshape(dp_size // 2, 2, mp_size), ("dz", "dc", "mp"))
    dp = ("dz", "dc")
    return jax.shard_map(
        per_device,
        mesh=inner,
        in_specs=(
            P(dp, "mp"),
            P(),
            P(dp, "mp"),
            P(dp, "mp"),
            P(dp, "mp"),
            P("mp"),
            P("mp"),
            P("mp"),
            P(),
            P(),
            P(),
            P(),
            P(dp, None, "mp"),
            P(dp, None, "mp"),
            P(dp, None, None, None, "mp"),
            P(dp, None),
        ),
        out_specs=(P(dp, "mp"), P(dp, None, None, None, "mp")),
        check_vma=False,
    )
```

```python
import math

import jax
import jax.numpy as jnp
from jax import lax
from jax.sharding import Mesh, PartitionSpec as P

HD = 128
CAP = 2
MAX_REQUEST = 3072


NEG_BIG = -1e30
EPSILON = 1e-06
THETA = 1000000.0


def rotary(values, positions):
    head_dim = values.shape[-1]
    half_dim = head_dim // 2
    frequency = jnp.exp(
        -jnp.arange(half_dim, dtype=jnp.float32) * (2.0 / head_dim) * math.log(THETA)
    )
    angles = positions[:, None] * frequency[None, :]
    cosine = jnp.concatenate([jnp.cos(angles), jnp.cos(angles)], axis=-1)[:, None, :]
    sine_part = jnp.concatenate([jnp.sin(angles), jnp.sin(angles)], axis=-1)[:, None, :]
    first_half = values[..., :half_dim]
    second_half = values[..., half_dim:]
    turned = jnp.concatenate([-second_half, first_half], axis=-1)
    return values * cosine + turned * sine_part


def request_index(rows_here, ends_at):
    return jnp.sum((rows_here[:, None] >= ends_at[None, :]).astype(jnp.int32), axis=1)


def token_table(global_rows, request_lens, request_group, prompt_lens):
    ends_at = jnp.cumsum(request_lens)
    starts_at = ends_at - request_lens
    request_of = request_index(global_rows, ends_at)
    one_hot = request_of[:, None] == jnp.arange(request_lens.shape[0], dtype=jnp.int32)[None, :]
    first_row = jnp.sum(jnp.where(one_hot, starts_at[None, :], 0), axis=1)
    group_of = jnp.sum(jnp.where(one_hot, request_group[None, :], 0), axis=1)
    group_hot = group_of[:, None] == jnp.arange(prompt_lens.shape[0], dtype=jnp.int32)[None, :]
    prefix_of = jnp.sum(jnp.where(group_hot, prompt_lens[None, :], 0), axis=1)
    positions = (prefix_of + global_rows - first_row).astype(jnp.float32)
    return (request_of, group_hot, positions, ends_at)


def prompt_mask(prompt_table, prompt_lens, block_count, block_size):
    blocks = jnp.arange(block_count, dtype=jnp.int32)
    matching = prompt_table[:, :, None] == blocks[None, None, :]
    present = jnp.any(matching, axis=1)
    slot_no = jnp.sum(
        jnp.where(matching, jnp.arange(prompt_table.shape[1], dtype=jnp.int32)[None, :, None], 0),
        axis=1,
    )
    within = (
        slot_no[:, :, None] * block_size + jnp.arange(block_size, dtype=jnp.int32)[None, None, :]
    )
    allowed = present[:, :, None] & (within < prompt_lens[:, None, None])
    return allowed.reshape(prompt_table.shape[0], block_count * block_size)


def attend(current, queries, keys_flat, values_flat, allowed, score_scale):
    best_score, total_sum, accumulated = current
    scores = (
        jnp.einsum("kgqd,skd->kgqs", queries, keys_flat, preferred_element_type=jnp.float32)
        * score_scale
    )
    masked = allowed[None, None, :, :]
    scores = jnp.where(masked, scores, NEG_BIG)
    new_best = jnp.maximum(best_score, jnp.max(scores, axis=-1))
    weights = jnp.where(masked, jnp.exp(scores - new_best[..., None]), 0.0)
    factor = jnp.exp(best_score - new_best)
    total_sum = total_sum * factor + jnp.sum(weights, axis=-1)
    accumulated = accumulated * factor[..., None] + jnp.einsum(
        "kgqs,skd->kgqd",
        weights.astype(jnp.bfloat16),
        values_flat,
        preferred_element_type=jnp.float32,
    )
    return (new_best, total_sum, accumulated)


def dp_index():
    return lax.axis_index("dz") * lax.axis_size("dc") + lax.axis_index("dc")


def pack_cache(prev_cache, dest_device):
    blocks_here = prev_cache.shape[0]
    devices = lax.axis_size("dz") * lax.axis_size("dc")
    slot_count = devices * CAP
    target = dest_device[:, 0]
    same_target = target[:, None] == target[None, :]
    earlier = (
        jnp.arange(blocks_here, dtype=jnp.int32)[None, :]
        < jnp.arange(blocks_here, dtype=jnp.int32)[:, None]
    )
    block_rank = jnp.sum((same_target & earlier).astype(jnp.int32), axis=1)
    slot_device = jnp.arange(slot_count, dtype=jnp.int32) // CAP
    slot_rank = jnp.arange(slot_count, dtype=jnp.int32) % CAP
    matches = (target[None, :] == slot_device[:, None]) & (
        block_rank[None, :] == slot_rank[:, None]
    )
    filled = jnp.any(matches, axis=1)
    source = jnp.sum(
        jnp.where(matches, jnp.arange(blocks_here, dtype=jnp.int32)[None, :], 0), axis=1
    )
    packed = jnp.take(prev_cache, source, axis=0, mode="clip")
    slot_flags = filled.astype(jnp.bfloat16)
    return packed, slot_flags


def swap_flags(slot_flags):
    return lax.all_to_all(slot_flags, ("dz", "dc"), split_axis=0, concat_axis=0, tiled=True)


def unpack_cache(packed, arrived_flags):
    blocks_here = packed.shape[0] // CAP
    slot_count = packed.shape[0]
    arrived = lax.all_to_all(packed, ("dz", "dc"), split_axis=0, concat_axis=0, tiled=True)
    arrived_live = arrived_flags > 0.5
    order_no = jnp.cumsum(arrived_live.astype(jnp.int32)) - 1
    picked = arrived_live[None, :] & (
        order_no[None, :] == jnp.arange(blocks_here, dtype=jnp.int32)[:, None]
    )
    chosen = jnp.sum(jnp.where(picked, jnp.arange(slot_count, dtype=jnp.int32)[None, :], 0), axis=1)
    return jnp.take(arrived, chosen, axis=0, mode="clip")


def per_device(
    hidden,
    norm_gain,
    query_weight,
    key_weight,
    value_weight,
    query_bias,
    key_bias,
    value_bias,
    request_lens,
    request_group,
    prompt_lens,
    prompt_table,
    pool_keys,
    pool_values,
    prev_cache,
    dest_device,
):
    row_count = hidden.shape[0]
    me = dp_index()
    side = lax.axis_index("dc")
    sides = lax.axis_size("dc")
    global_rows = me * row_count + jnp.arange(row_count, dtype=jnp.int32)
    request_of, group_hot, positions, ends_at = token_table(
        global_rows, request_lens, request_group, prompt_lens
    )
    mp_size = lax.axis_size("mp")
    spread = jnp.broadcast_to(hidden[None], (mp_size,) + hidden.shape)
    pieces = lax.all_to_all(spread, "mp", split_axis=0, concat_axis=0, tiled=True)
    packed, slot_flags = pack_cache(prev_cache, dest_device)
    arrived_flags = swap_flags(slot_flags)
    pieces, packed, arrived_flags = lax.optimization_barrier((pieces, packed, arrived_flags))
    q_cols = query_weight.shape[1]
    k_cols = key_weight.shape[1]
    block_rows = query_weight.shape[0]
    pool_here = jnp.concatenate([pool_keys, pool_values], axis=2).reshape(block_rows, -1)
    weights_here = jnp.concatenate([query_weight, key_weight, value_weight, pool_here], axis=1)
    weights_all = lax.all_gather(weights_here, ("dz", "dc"), axis=0, tiled=True)
    proj_cols = q_cols + 2 * k_cols
    pool_all = weights_all[:, proj_cols:].reshape(
        (-1,) + pool_keys.shape[1:2] + (2 * pool_keys.shape[2],)
    )
    as_float = pieces.astype(jnp.float32)
    inverse = lax.rsqrt(
        jnp.mean(jnp.sum(as_float * as_float, axis=2), axis=0)[None, :, None] / pieces.shape[2]
        + EPSILON
    )
    gain = norm_gain.astype(jnp.float32).reshape(mp_size, 1, -1)
    normed = (as_float * inverse * gain).astype(jnp.bfloat16)
    normed = lax.optimization_barrier(normed.transpose(1, 0, 2).reshape(row_count, -1))
    proj = jnp.dot(normed, weights_all, preferred_element_type=jnp.float32)
    query_proj = proj[:, :q_cols] + query_bias.astype(jnp.float32)[None, :]
    key_proj = proj[:, q_cols:q_cols + k_cols] + key_bias.astype(jnp.float32)[None, :]
    value_proj = proj[:, q_cols + k_cols:proj_cols] + value_bias.astype(jnp.float32)[None, :]
    local_heads = query_proj.shape[1] // HD
    local_kv = key_proj.shape[1] // HD
    group_size = local_heads // local_kv
    queries = rotary(query_proj.reshape(row_count, local_heads, HD), positions).astype(jnp.bfloat16)
    queries = queries.reshape(row_count, local_kv, group_size, HD).transpose(1, 2, 0, 3)
    keys_new = (
        rotary(key_proj.reshape(row_count, local_kv, HD), positions)
        .astype(jnp.bfloat16)
        .reshape(row_count, local_kv * HD)
    )
    values_new = value_proj.astype(jnp.bfloat16)
    span_here = jnp.concatenate([keys_new, values_new], axis=1)
    span_all = lax.all_gather(span_here, ("dz", "dc"), axis=0, tiled=True)
    packed, arrived_flags, span_all = lax.optimization_barrier((packed, arrived_flags, span_all))
    decode_cache = unpack_cache(packed, arrived_flags)
    score_scale = HD ** (-0.5)
    carried = (
        jnp.full((local_kv, group_size, row_count), NEG_BIG, jnp.float32),
        jnp.zeros((local_kv, group_size, row_count), jnp.float32),
        jnp.zeros((local_kv, group_size, row_count, HD), jnp.float32),
    )
    block_size = pool_all.shape[1]
    blocks_here = pool_all.shape[0]
    kv_width = local_kv * HD
    allowed_group = prompt_mask(prompt_table, prompt_lens, blocks_here, block_size)
    allowed = jnp.any(group_hot[:, :, None] & allowed_group[None, :, :], axis=1)
    keys_flat = pool_all[:, :, :kv_width].reshape(blocks_here * block_size, local_kv, HD)
    values_flat = pool_all[:, :, kv_width:].reshape(blocks_here * block_size, local_kv, HD)
    carried = attend(carried, queries, keys_flat, values_flat, allowed, score_scale)
    key_count = span_all.shape[0]
    window = min(key_count, MAX_REQUEST + row_count)
    window = -(-window // row_count) * row_count
    window_start = jnp.maximum((me + 1) * row_count - window, 0)
    span_window = lax.dynamic_slice_in_dim(span_all, window_start, window, axis=0)
    key_rows = window_start + jnp.arange(window, dtype=jnp.int32)
    key_request = request_index(key_rows, ends_at)
    span_allowed = (request_of[:, None] == key_request[None, :]) & (
        key_rows[None, :] <= global_rows[:, None]
    )
    span_keys_flat = span_window[:, :kv_width].reshape(window, local_kv, HD)
    span_values_flat = span_window[:, kv_width:].reshape(window, local_kv, HD)
    carried = attend(
        carried, queries, span_keys_flat, span_values_flat, span_allowed, score_scale
    )
    best_score, total_sum, accumulated = carried
    output = accumulated / total_sum[..., None]
    context = output.transpose(2, 0, 1, 3).reshape(row_count, local_heads * HD).astype(jnp.bfloat16)
    return (context, decode_cache)


def solution(mesh):
    dp_size, mp_size = mesh.devices.shape
    inner = Mesh(mesh.devices.reshape(dp_size // 2, 2, mp_size), ("dz", "dc", "mp"))
    dp = ("dz", "dc")
    return jax.shard_map(
        per_device,
        mesh=inner,
        in_specs=(
            P(dp, "mp"),
            P(),
            P(dp, "mp"),
            P(dp, "mp"),
            P(dp, "mp"),
            P("mp"),
            P("mp"),
            P("mp"),
            P(),
            P(),
            P(),
            P(),
            P(dp, None, "mp"),
            P(dp, None, "mp"),
            P(dp, None, None, None, "mp"),
            P(dp, None),
        ),
        out_specs=(P(dp, "mp"), P(dp, None, None, None, "mp")),
        check_vma=False,
    )
```
